128 devices in a mesh: mom: 16 (over z, y), hist: 8 (over x, core).
Axes of the slice: x: 4, y: 4, z: 4, core: 2. Of those that a mesh axis runs over, the one named last changes fastest.
Arguments:
- hist_panel: float32 [2, 128, 1024, 1024], P(None, 'mom', 'hist')
- free_rows: float32 [2, 128, 4, 1024], P(None, 'mom', None, 'hist'), may hold values from -6 to 6
- screened: float32 [2, 128, 4, 1024], P(None, 'mom', None, 'hist'), may hold values from -0.5 to 0.5
Outputs:
- new_rows: float32 [2, 128, 4, 1024], P(None, 'mom', None, 'hist')
- change_norms: float32 [6], replicated
The draws below stay inside these ranges and needn't reach their ends.
All inputs are finite; a program needn't handle non-finite values.
Results may differ from the reference program's by a relative error of at most 0.0001.
Values sent between devices are 32-bit elements; how exact they have to be, the bound alone decides.
No kernel may reach another device: no remote copies, remote signals or barrier semaphores. Data moves between devices by JAX's collectives and lax.ppermute only.
A program may use at most 64 MiB of HBM per device.

```python
import jax
import jax.numpy as jnp
from jax import lax

K = 128
R = 4
ITERS = 6
H = 1024


def draw_hist_panel(key, part):
    points = jnp.arange(K, dtype=jnp.float32) / (K - 1.0)
    entries = jnp.clip(jax.random.normal(key, (2, K, H, H), jnp.float32), -6.0, 6.0)
    ramp = jnp.exp(jnp.log(3.0) * points)
    return entries * (ramp[None, :, None, None] / jnp.sqrt(H * 1.0))


def block_levels(key, extent, shards, smallest, largest):
    level, own = 1.0, jax.random.fold_in(key, 6)
    for dim, blocks in shards:
        steps = jnp.exp(jax.random.uniform(jax.random.fold_in(own, dim), (blocks,), jnp.float32, smallest / len(shards), largest / len(shards)))
        level = level * jnp.repeat(steps, extent[dim] // blocks).reshape([-1 if axis == dim else 1 for axis in range(len(extent))])
    return level


def bell_draw(stream_key, dims, spread, most, shards=(), kind=jnp.bfloat16):
    values = spread * jax.random.normal(stream_key, dims, jnp.float32)
    if shards:
        values = values * block_levels(stream_key, dims, shards, -0.22, 0.18)
    return jnp.clip(values, -most, most).astype(kind)


def setup_inputs(seed: int = 0) -> dict:
    arg_keys = jax.random.split(jax.random.key(seed), 4)
    hist_panel = draw_hist_panel(jax.random.fold_in(arg_keys[3], 71), 0)
    free_rows = bell_draw(arg_keys[1], (2, K, R, H), 1.0, 6.0, ((1, 16), (3, 8)), jnp.float32)
    screened = bell_draw(arg_keys[2], (2, K, R, H), K ** -0.5, 0.5, ((1, 16), (3, 8)), jnp.float32)
    return dict(hist_panel=hist_panel, free_rows=free_rows, screened=screened)


step_size = 0.25

def contract(left, right):
    return jnp.einsum('krs,kst->krt', left, right, precision=lax.Precision.HIGHEST)

def reference(hist_panel, free_rows, screened):
    screen_hat = jnp.fft.fft(screened[0] + 1j * screened[1], axis=0)
    green_real = free_rows[0]
    green_imag = free_rows[1]
    deltas = []
    for turn in range(ITERS):
        green_cplx = green_real + 1j * green_imag
        sigma_cplx = 1j * jnp.fft.ifft(jnp.fft.fft(green_cplx, axis=0) * screen_hat, axis=0)
        sigma_real = jnp.real(sigma_cplx)
        sigma_imag = jnp.imag(sigma_cplx)
        integral_real = contract(sigma_real, hist_panel[0]) - contract(sigma_imag, hist_panel[1])
        integral_imag = contract(sigma_real, hist_panel[1]) + contract(sigma_imag, hist_panel[0])
        change_real = free_rows[0] + step_size * integral_real - green_real
        change_imag = free_rows[1] + step_size * integral_imag - green_imag
        total = jnp.sum(change_real * change_real) + jnp.sum(change_imag * change_imag)
        delta = jnp.sqrt(total / (2.0 * K * R * H))
        deltas.append(delta)
        green_real = green_real + change_real / (1.0 + delta)
        green_imag = green_imag + change_imag / (1.0 + delta)
    return (jnp.stack([green_real, green_imag]), jnp.stack(deltas))
```

```python
import math

import jax
import jax.numpy as jnp
from jax import lax
from jax.sharding import PartitionSpec as P

K = 128
R = 4
ITERS = 6


step_size = 0.25
HIGHEST = lax.Precision.HIGHEST


def tables(rows):
    points = jnp.arange(K, dtype=jnp.int32)
    product = rows[:, None] * points[None, :] % K
    phase = product.astype(jnp.float32) * (2.0 * math.pi / K)
    return (jnp.cos(phase), jnp.sin(phase))


def mm(table, field):
    return jnp.dot(table, field, precision=HIGHEST)


def dft(cosine, sine, real, imag):
    both = jnp.concatenate([real, imag], axis=1)
    cr = mm(cosine, both)
    sr = mm(sine, both)
    n = real.shape[1]
    return (cr[:, :n] + sr[:, n:], cr[:, n:] - sr[:, :n])


def gather_rows(flat, extra):
    pad = jnp.zeros((128,), flat.dtype).at[0].set(extra)
    packed = jnp.concatenate([flat, pad])
    got = lax.all_gather(packed, "mom", tiled=False)
    n = flat.shape[0]
    return got[:, :n], jnp.sum(got[:, n])


def to_full_k(rows, lead, k_local, cols):
    g = rows.reshape(rows.shape[0], lead, k_local, R * cols)
    g = jnp.transpose(g, (1, 0, 2, 3))
    return g.reshape(lead, rows.shape[0] * k_local, R * cols)


def hist_reduce(partial, extra, hist_n):
    two, kl, rr, h = partial.shape
    cols = h // hist_n
    x = partial.reshape(two, kl, rr, hist_n, cols)
    x = jnp.transpose(x, (3, 0, 1, 2, 4)).reshape(hist_n, two * kl * rr * cols)
    pad = jnp.zeros((hist_n, 128), x.dtype).at[:, 0].set(extra)
    x = jnp.concatenate([x, pad], axis=1)
    y = lax.all_to_all(x, "hist", 0, 0, tiled=True)
    s = jnp.sum(y, axis=0)
    n = two * kl * rr * cols
    return s[:n].reshape(two, kl, rr, cols), s[n]


def shards(hist_panel, free_rows, screened):
    _, k_local, _, cols = free_rows.shape
    hist_n = hist_panel.shape[3] // cols
    full_hist = hist_panel.shape[3]
    mom_i = lax.axis_index("mom")
    cosine, sine = tables(jnp.arange(K, dtype=jnp.int32))
    own = mom_i * k_local + jnp.arange(k_local, dtype=jnp.int32)
    cos_own, sin_own = tables(own)
    cos_own = cos_own / K
    sin_own = sin_own / K
    nb = 2 * k_local * R * cols

    def sigma_of(full):
        hr, hi = dft(cosine, sine, full[0], full[1])
        pr = hr * screen_hat[0] - hi * screen_hat[1]
        pi = hr * screen_hat[1] + hi * screen_hat[0]
        both = jnp.concatenate([pr, pi], axis=1)
        cb = mm(cos_own, both)
        sb = mm(sin_own, both)
        n = pr.shape[1]
        back_real = cb[:, :n] - sb[:, n:]
        back_imag = cb[:, n:] + sb[:, :n]
        return jnp.stack([-back_imag, back_real]).reshape(2, k_local, R, cols)

    def contract(sigma):
        x = jnp.concatenate([sigma[0], sigma[1]], axis=1)
        a = jnp.einsum("kxs,kst->kxt", x, hist_panel[0], precision=HIGHEST)
        b = jnp.einsum("kxs,kst->kxt", x, hist_panel[1], precision=HIGHEST)
        real = a[:, :R] - b[:, R:]
        imag = b[:, :R] + a[:, R:]
        return jnp.stack([real, imag])

    first = jnp.concatenate([screened.reshape(-1), free_rows.reshape(-1)])
    rows, _ = gather_rows(first, jnp.float32(0.0))
    rows = rows.reshape(rows.shape[0], 2, nb)
    screen_full = to_full_k(rows[:, 0], 2, k_local, cols)
    green_full = to_full_k(rows[:, 1], 2, k_local, cols)
    screen_hat = dft(cosine, sine, screen_full[0], screen_full[1])

    integral, _ = hist_reduce(contract(sigma_of(green_full)), jnp.float32(0.0), hist_n)
    green = free_rows
    deltas = []
    for turn in range(ITERS):
        change = free_rows + step_size * integral - green
        local = jnp.sum(change * change)
        if turn + 1 < ITERS:
            rows, mom_sum = gather_rows(change.reshape(-1), local)
            full = to_full_k(rows, 2, k_local, cols)
            step, total = hist_reduce(contract(sigma_of(full)), mom_sum, hist_n)
        else:
            n_dev = lax.axis_size(("mom", "hist"))
            spread = jnp.broadcast_to(local, (n_dev, 1))
            total = jnp.sum(lax.all_to_all(spread, ("mom", "hist"), 0, 0, tiled=True))
        delta = jnp.sqrt(total / (2.0 * K * R * full_hist))
        deltas.append(delta)
        green = green + change / (1.0 + delta)
        if turn + 1 < ITERS:
            integral = integral + step / (1.0 + delta)
    return (green, jnp.stack(deltas))


def solution(mesh):
    placed = (
        P(None, "mom", "hist", None),
        P(None, "mom", None, "hist"),
        P(None, "mom", None, "hist"),
    )
    return jax.shard_map(
        shards,
        mesh=mesh,
        in_specs=placed,
        out_specs=(P(None, "mom", None, "hist"), P()),
        check_vma=False,
    )
```

```python
import math

import jax
import jax.numpy as jnp
from jax import lax
from jax.sharding import PartitionSpec as P

K = 128
R = 4
ITERS = 6


step_size = 0.25
HIGHEST = lax.Precision.HIGHEST


def tables(rows):
    points = jnp.arange(K, dtype=jnp.int32)
    product = rows[:, None] * points[None, :] % K
    phase = product.astype(jnp.float32) * (2.0 * math.pi / K)
    return (jnp.cos(phase), jnp.sin(phase))


def mm(table, field):
    return jnp.dot(table, field, precision=HIGHEST)


def dft(cosine, sine, real, imag):
    both = jnp.concatenate([real, imag], axis=1)
    cr = mm(cosine, both)
    sr = mm(sine, both)
    n = real.shape[1]
    return (cr[:, :n] + sr[:, n:], cr[:, n:] - sr[:, :n])


def gather_rows(flat, extra):
    pad = jnp.zeros((128,), flat.dtype).at[0].set(extra)
    packed = jnp.concatenate([flat, pad])
    got = lax.all_gather(packed, "mom", tiled=False)
    n = flat.shape[0]
    return got[:, :n], jnp.sum(got[:, n])


def to_full_k(rows, lead, k_local, cols):
    g = rows.reshape(rows.shape[0], lead, k_local, R * cols)
    g = jnp.transpose(g, (1, 0, 2, 3))
    return g.reshape(lead, rows.shape[0] * k_local, R * cols)


def hist_reduce(partial, extra, hist_n):
    two, kl, rr, h = partial.shape
    cols = h // hist_n
    x = partial.reshape(two, kl, rr, hist_n, cols)
    x = jnp.transpose(x, (3, 0, 1, 2, 4)).reshape(hist_n, two * kl * rr * cols)
    pad = jnp.zeros((hist_n, 128), x.dtype).at[:, 0].set(extra)
    x = jnp.concatenate([x, pad], axis=1)
    y = lax.all_to_all(x, "hist", 0, 0, tiled=True)
    s = jnp.sum(y, axis=0)
    n = two * kl * rr * cols
    return s[:n].reshape(two, kl, rr, cols), s[n]


def shards(hist_panel, free_rows, screened):
    _, k_local, _, cols = free_rows.shape
    hist_n = hist_panel.shape[3] // cols
    full_hist = hist_panel.shape[3]
    mom_i = lax.axis_index("mom")
    cosine, sine = tables(jnp.arange(K, dtype=jnp.int32))
    own = mom_i * k_local + jnp.arange(k_local, dtype=jnp.int32)
    cos_own, sin_own = tables(own)
    cos_own = cos_own / K
    sin_own = sin_own / K
    nb = 2 * k_local * R * cols

    def sigma_of(full):
        hr, hi = dft(cosine, sine, full[0], full[1])
        pr = hr * screen_hat[0] - hi * screen_hat[1]
        pi = hr * screen_hat[1] + hi * screen_hat[0]
        both = jnp.concatenate([pr, pi], axis=1)
        cb = mm(cos_own, both)
        sb = mm(sin_own, both)
        n = pr.shape[1]
        back_real = cb[:, :n] - sb[:, n:]
        back_imag = cb[:, n:] + sb[:, :n]
        return jnp.stack([-back_imag, back_real]).reshape(2, k_local, R, cols)

    def contract(sigma):
        x = jnp.concatenate([sigma[0], sigma[1]], axis=1)
        a = jnp.einsum("kxs,kst->kxt", x, hist_panel[0], precision=lax.Precision.HIGH)
        b = jnp.einsum("kxs,kst->kxt", x, hist_panel[1], precision=lax.Precision.HIGH)
        real = a[:, :R] - b[:, R:]
        imag = b[:, :R] + a[:, R:]
        return jnp.stack([real, imag])

    first = jnp.concatenate([screened.reshape(-1), free_rows.reshape(-1)])
    rows, _ = gather_rows(first, jnp.float32(0.0))
    rows = rows.reshape(rows.shape[0], 2, nb)
    screen_full = to_full_k(rows[:, 0], 2, k_local, cols)
    green_full = to_full_k(rows[:, 1], 2, k_local, cols)
    screen_hat = dft(cosine, sine, screen_full[0], screen_full[1])

    integral, _ = hist_reduce(contract(sigma_of(green_full)), jnp.float32(0.0), hist_n)
    green = free_rows
    deltas = []
    for turn in range(ITERS):
        change = free_rows + step_size * integral - green
        local = jnp.sum(change * change)
        if turn + 1 < ITERS:
            rows, mom_sum = gather_rows(change.reshape(-1), local)
            full = to_full_k(rows, 2, k_local, cols)
            step, total = hist_reduce(contract(sigma_of(full)), mom_sum, hist_n)
        else:
            n_dev = lax.axis_size(("mom", "hist"))
            spread = jnp.broadcast_to(local, (n_dev, 1))
            total = jnp.sum(lax.all_to_all(spread, ("mom", "hist"), 0, 0, tiled=True))
        delta = jnp.sqrt(total / (2.0 * K * R * full_hist))
        deltas.append(delta)
        green = green + change / (1.0 + delta)
        if turn + 1 < ITERS:
            integral = integral + step / (1.0 + delta)
    return (green, jnp.stack(deltas))


def solution(mesh):
    placed = (
        P(None, "mom", "hist", None),
        P(None, "mom", None, "hist"),
        P(None, "mom", None, "hist"),
    )
    return jax.shard_map(
        shards,
        mesh=mesh,
        in_specs=placed,
        out_specs=(P(None, "mom", None, "hist"), P()),
        check_vma=False,
    )
```

```python
import math

import jax
import jax.numpy as jnp
from jax import lax
from jax.sharding import PartitionSpec as P

K = 128
R = 4
ITERS = 6


step_size = 0.25
HIGHEST = lax.Precision.HIGHEST


def tables(rows):
    points = jnp.arange(K, dtype=jnp.int32)
    product = rows[:, None] * points[None, :] % K
    phase = product.astype(jnp.float32) * (2.0 * math.pi / K)
    return (jnp.cos(phase), jnp.sin(phase))


def mm(table, field):
    return jnp.dot(table, field, precision=HIGHEST)


def dft(cosine, sine, real, imag):
    both = jnp.concatenate([real, imag], axis=1)
    cr = mm(cosine, both)
    sr = mm(sine, both)
    n = real.shape[1]
    return (cr[:, :n] + sr[:, n:], cr[:, n:] - sr[:, :n])


def gather_rows(flat, extra):
    pad = jnp.zeros((128,), flat.dtype).at[0].set(extra)
    packed = jnp.concatenate([flat, pad])
    n_mom = lax.axis_size("mom")
    got = lax.all_to_all(jnp.broadcast_to(packed, (n_mom,) + packed.shape), "mom", 0, 0, tiled=True)
    n = flat.shape[0]
    return got[:, :n], jnp.sum(got[:, n])


def to_full_k(rows, lead, k_local, cols):
    g = rows.reshape(rows.shape[0], lead, k_local, R * cols)
    g = jnp.transpose(g, (1, 0, 2, 3))
    return g.reshape(lead, rows.shape[0] * k_local, R * cols)


def hist_reduce(partial, extra, hist_n):
    two, kl, rr, h = partial.shape
    cols = h // hist_n
    x = partial.reshape(two, kl, rr, hist_n, cols)
    x = jnp.transpose(x, (3, 0, 1, 2, 4)).reshape(hist_n, two * kl * rr * cols)
    pad = jnp.zeros((hist_n, 128), x.dtype).at[:, 0].set(extra)
    x = jnp.concatenate([x, pad], axis=1)
    y = lax.all_to_all(x, "hist", 0, 0, tiled=True)
    s = jnp.sum(y, axis=0)
    n = two * kl * rr * cols
    return s[:n].reshape(two, kl, rr, cols), s[n]


def shards(hist_panel, free_rows, screened):
    _, k_local, _, cols = free_rows.shape
    hist_n = hist_panel.shape[3] // cols
    full_hist = hist_panel.shape[3]
    mom_i = lax.axis_index("mom")
    cosine, sine = tables(jnp.arange(K, dtype=jnp.int32))
    own = mom_i * k_local + jnp.arange(k_local, dtype=jnp.int32)
    cos_own, sin_own = tables(own)
    cos_own = cos_own / K
    sin_own = sin_own / K
    nb = 2 * k_local * R * cols

    def sigma_of(full):
        hr, hi = dft(cosine, sine, full[0], full[1])
        pr = hr * screen_hat[0] - hi * screen_hat[1]
        pi = hr * screen_hat[1] + hi * screen_hat[0]
        both = jnp.concatenate([pr, pi], axis=1)
        cb = mm(cos_own, both)
        sb = mm(sin_own, both)
        n = pr.shape[1]
        back_real = cb[:, :n] - sb[:, n:]
        back_imag = cb[:, n:] + sb[:, :n]
        return jnp.stack([-back_imag, back_real]).reshape(2, k_local, R, cols)

    def contract(sigma):
        x = jnp.concatenate([sigma[0], sigma[1]], axis=1)
        a = jnp.einsum("kxs,kst->kxt", x, hist_panel[0], precision=HIGHEST)
        b = jnp.einsum("kxs,kst->kxt", x, hist_panel[1], precision=HIGHEST)
        real = a[:, :R] - b[:, R:]
        imag = b[:, :R] + a[:, R:]
        return jnp.stack([real, imag])

    first = jnp.concatenate([screened.reshape(-1), free_rows.reshape(-1)])
    rows, _ = gather_rows(first, jnp.float32(0.0))
    rows = rows.reshape(rows.shape[0], 2, nb)
    screen_full = to_full_k(rows[:, 0], 2, k_local, cols)
    green_full = to_full_k(rows[:, 1], 2, k_local, cols)
    screen_hat = dft(cosine, sine, screen_full[0], screen_full[1])

    integral, _ = hist_reduce(contract(sigma_of(green_full)), jnp.float32(0.0), hist_n)
    green = free_rows
    deltas = []
    for turn in range(ITERS):
        change = free_rows + step_size * integral - green
        local = jnp.sum(change * change)
        if turn + 1 < ITERS:
            rows, mom_sum = gather_rows(change.reshape(-1), local)
            full = to_full_k(rows, 2, k_local, cols)
            step, total = hist_reduce(contract(sigma_of(full)), mom_sum, hist_n)
        else:
            n_dev = lax.axis_size(("mom", "hist"))
            spread = jnp.broadcast_to(local, (n_dev, 1))
            total = jnp.sum(lax.all_to_all(spread, ("mom", "hist"), 0, 0, tiled=True))
        delta = jnp.sqrt(total / (2.0 * K * R * full_hist))
        deltas.append(delta)
        green = green + change / (1.0 + delta)
        if turn + 1 < ITERS:
            integral = integral + step / (1.0 + delta)
    return (green, jnp.stack(deltas))


def solution(mesh):
    placed = (
        P(None, "mom", "hist", None),
        P(None, "mom", None, "hist"),
        P(None, "mom", None, "hist"),
    )
    return jax.shard_map(
        shards,
        mesh=mesh,
        in_specs=placed,
        out_specs=(P(None, "mom", None, "hist"), P()),
        check_vma=False,
    )
```

```python
import math

import jax
import jax.numpy as jnp
from jax import lax
from jax.sharding import PartitionSpec as P

K = 128
R = 4
ITERS = 6


step_size = 0.25
HIGHEST = lax.Precision.HIGHEST


def tables(rows):
    points = jnp.arange(K, dtype=jnp.int32)
    product = rows[:, None] * points[None, :] % K
    phase = product.astype(jnp.float32) * (2.0 * math.pi / K)
    return (jnp.cos(phase), jnp.sin(phase))


def mm(table, field):
    return jnp.dot(table, field, precision=HIGHEST)


def dft(cosine, sine, real, imag):
    both = jnp.concatenate([real, imag], axis=1)
    cr = mm(cosine, both)
    sr = mm(sine, both)
    n = real.shape[1]
    return (cr[:, :n] + sr[:, n:], cr[:, n:] - sr[:, :n])


def gather_rows(flat, extra):
    pad = jnp.zeros((128,), flat.dtype).at[0].set(extra)
    packed = jnp.concatenate([flat, pad])
    n_mom = lax.axis_size("mom")
    got = lax.all_to_all(jnp.broadcast_to(packed, (n_mom,) + packed.shape), "mom", 0, 0, tiled=True)
    n = flat.shape[0]
    return got[:, :n], jnp.sum(got[:, n])


def to_full_k(rows, lead, k_local, cols):
    g = rows.reshape(rows.shape[0], lead, k_local, R * cols)
    g = jnp.transpose(g, (1, 0, 2, 3))
    return g.reshape(lead, rows.shape[0] * k_local, R * cols)


def hist_reduce(partial, extra, hist_n):
    two, kl, rr, h = partial.shape
    cols = h // hist_n
    x = partial.reshape(two, kl, rr, hist_n, cols)
    x = jnp.transpose(x, (3, 0, 1, 2, 4)).reshape(hist_n, two * kl * rr * cols)
    pad = jnp.zeros((hist_n, 128), x.dtype).at[:, 0].set(extra)
    x = jnp.concatenate([x, pad], axis=1)
    y = lax.all_to_all(x, "hist", 0, 0, tiled=True)
    s = jnp.sum(y, axis=0)
    n = two * kl * rr * cols
    return s[:n].reshape(two, kl, rr, cols), s[n]


def shards(hist_panel, free_rows, screened):
    _, k_local, _, cols = free_rows.shape
    hist_n = hist_panel.shape[3] // cols
    full_hist = hist_panel.shape[3]
    mom_i = lax.axis_index("mom")
    cosine, sine = tables(jnp.arange(K, dtype=jnp.int32))
    own = mom_i * k_local + jnp.arange(k_local, dtype=jnp.int32)
    cos_own, sin_own = tables(own)
    cos_own = cos_own / K
    sin_own = sin_own / K
    nb = 2 * k_local * R * cols

    def sigma_of(full):
        hr, hi = dft(cosine, sine, full[0], full[1])
        pr = hr * screen_hat[0] - hi * screen_hat[1]
        pi = hr * screen_hat[1] + hi * screen_hat[0]
        both = jnp.concatenate([pr, pi], axis=1)
        cb = mm(cos_own, both)
        sb = mm(sin_own, both)
        n = pr.shape[1]
        back_real = cb[:, :n] - sb[:, n:]
        back_imag = cb[:, n:] + sb[:, :n]
        return jnp.stack([-back_imag, back_real]).reshape(2, k_local, R, cols)

    def contract(sigma):
        x = jnp.concatenate([sigma[0], sigma[1]], axis=1)
        a = jnp.einsum("kxs,kst->kxt", x, hist_panel[0], precision=HIGHEST)
        b = jnp.einsum("kxs,kst->kxt", x, hist_panel[1], precision=HIGHEST)
        real = a[:, :R] - b[:, R:]
        imag = b[:, :R] + a[:, R:]
        return jnp.stack([real, imag])

    first = jnp.concatenate([screened.reshape(-1), free_rows.reshape(-1)])
    rows, _ = gather_rows(first, jnp.float32(0.0))
    rows = rows.reshape(rows.shape[0], 2, nb)
    screen_full = to_full_k(rows[:, 0], 2, k_local, cols)
    green_full = to_full_k(rows[:, 1], 2, k_local, cols)
    screen_hat = dft(cosine, sine, screen_full[0], screen_full[1])

    integral, _ = hist_reduce(contract(sigma_of(green_full)), jnp.float32(0.0), hist_n)
    def correction(turn, carry):
        green, integral, deltas = carry
        change = free_rows + step_size * integral - green
        local = jnp.sum(change * change)
        rows, mom_sum = gather_rows(change.reshape(-1), local)
        full = to_full_k(rows, 2, k_local, cols)
        step, total = hist_reduce(contract(sigma_of(full)), mom_sum, hist_n)
        delta = jnp.sqrt(total / (2.0 * K * R * full_hist))
        deltas = lax.dynamic_update_slice(deltas, delta[None], (turn,))
        green = green + change / (1.0 + delta)
        integral = integral + step / (1.0 + delta)
        return (green, integral, deltas)

    carry = (free_rows, integral, jnp.zeros((ITERS,), jnp.float32))
    green, integral, deltas = lax.fori_loop(0, ITERS - 1, correction, carry)
    change = free_rows + step_size * integral - green
    local = jnp.sum(change * change)
    n_dev = lax.axis_size(("mom", "hist"))
    spread = jnp.broadcast_to(local, (n_dev, 1))
    total = jnp.sum(lax.all_to_all(spread, ("mom", "hist"), 0, 0, tiled=True))
    delta = jnp.sqrt(total / (2.0 * K * R * full_hist))
    deltas = deltas.at[ITERS - 1].set(delta)
    green = green + change / (1.0 + delta)
    return (green, deltas)


def solution(mesh):
    placed = (
        P(None, "mom", "hist", None),
        P(None, "mom", None, "hist"),
        P(None, "mom", None, "hist"),
    )
    return jax.shard_map(
        shards,
        mesh=mesh,
        in_specs=placed,
        out_specs=(P(None, "mom", None, "hist"), P()),
        check_vma=False,
    )
```

```python
import math

import jax
import jax.numpy as jnp
from jax import lax
from jax.sharding import PartitionSpec as P

K = 128
R = 4
ITERS = 6


step_size = 0.25
HIGHEST = lax.Precision.HIGHEST


def tables(rows):
    points = jnp.arange(K, dtype=jnp.int32)
    product = rows[:, None] * points[None, :] % K
    phase = product.astype(jnp.float32) * (2.0 * math.pi / K)
    return (jnp.cos(phase), jnp.sin(phase))


def mm(table, field):
    return jnp.dot(table, field, precision=HIGHEST)


def dft(cosine, sine, real, imag):
    both = jnp.concatenate([real, imag], axis=1)
    cr = mm(cosine, both)
    sr = mm(sine, both)
    n = real.shape[1]
    return (cr[:, :n] + sr[:, n:], cr[:, n:] - sr[:, :n])


def gather_rows(block, extra):
    n_mom = lax.axis_size("mom")
    packed = jnp.concatenate([block, jnp.full((8, 128), extra, block.dtype)])
    got = lax.all_to_all(jnp.broadcast_to(packed, (n_mom,) + packed.shape), "mom", 0, 0, tiled=True)
    n = block.shape[0]
    return got[:, :n], jnp.sum(got[:, n, 0])


def to_full_k(rows, lead, k_local, cols):
    g = rows.reshape(rows.shape[0], lead, k_local, R * cols)
    g = jnp.transpose(g, (1, 0, 2, 3))
    return g.reshape(lead, rows.shape[0] * k_local, R * cols)


def hist_reduce(partial, extra, hist_n):
    two, kl, rr, h = partial.shape
    cols = h // hist_n
    x = partial.reshape(two, kl, rr, hist_n, cols)
    x = jnp.transpose(x, (3, 0, 1, 2, 4)).reshape(hist_n, two * kl * rr * cols // 128, 128)
    x = jnp.concatenate([x, jnp.full((hist_n, 8, 128), extra, x.dtype)], axis=1)
    y = lax.all_to_all(x, "hist", 0, 0, tiled=True)
    s = jnp.sum(y, axis=0)
    n = two * kl * rr * cols // 128
    return s[:n].reshape(two, kl, rr, cols), s[n, 0]


def shards(hist_panel, free_rows, screened):
    _, k_local, _, cols = free_rows.shape
    hist_n = hist_panel.shape[3] // cols
    full_hist = hist_panel.shape[3]
    mom_i = lax.axis_index("mom")
    cosine, sine = tables(jnp.arange(K, dtype=jnp.int32))
    own = mom_i * k_local + jnp.arange(k_local, dtype=jnp.int32)
    cos_own, sin_own = tables(own)
    cos_own = cos_own / K
    sin_own = sin_own / K
    nb = 2 * k_local * R * cols

    def sigma_of(full):
        hr, hi = dft(cosine, sine, full[0], full[1])
        pr = hr * screen_hat[0] - hi * screen_hat[1]
        pi = hr * screen_hat[1] + hi * screen_hat[0]
        both = jnp.concatenate([pr, pi], axis=1)
        cb = mm(cos_own, both)
        sb = mm(sin_own, both)
        n = pr.shape[1]
        back_real = cb[:, :n] - sb[:, n:]
        back_imag = cb[:, n:] + sb[:, :n]
        return jnp.stack([-back_imag, back_real]).reshape(2, k_local, R, cols)

    def contract(sigma):
        x = jnp.concatenate([sigma[0], sigma[1]], axis=1)
        a = jnp.einsum("kxs,kst->kxt", x, hist_panel[0], precision=HIGHEST)
        b = jnp.einsum("kxs,kst->kxt", x, hist_panel[1], precision=HIGHEST)
        real = a[:, :R] - b[:, R:]
        imag = b[:, :R] + a[:, R:]
        return jnp.stack([real, imag])

    first = jnp.concatenate([screened.reshape(-1, 128), free_rows.reshape(-1, 128)])
    rows, _ = gather_rows(first, jnp.float32(0.0))
    half = nb // 128
    screen_full = to_full_k(rows[:, :half], 2, k_local, cols)
    green_full = to_full_k(rows[:, half:], 2, k_local, cols)
    screen_hat = dft(cosine, sine, screen_full[0], screen_full[1])

    integral, _ = hist_reduce(contract(sigma_of(green_full)), jnp.float32(0.0), hist_n)
    def correction(turn, carry):
        green, integral, deltas = carry
        change = free_rows + step_size * integral - green
        local = jnp.sum(change * change)
        rows, mom_sum = gather_rows(change.reshape(-1, 128), local)
        full = to_full_k(rows, 2, k_local, cols)
        step, total = hist_reduce(contract(sigma_of(full)), mom_sum, hist_n)
        delta = jnp.sqrt(total / (2.0 * K * R * full_hist))
        deltas = lax.dynamic_update_slice(deltas, delta[None], (turn,))
        green = green + change / (1.0 + delta)
        integral = integral + step / (1.0 + delta)
        return (green, integral, deltas)

    carry = (free_rows, integral, jnp.zeros((ITERS,), jnp.float32))
    green, integral, deltas = lax.fori_loop(0, ITERS - 1, correction, carry)
    change = free_rows + step_size * integral - green
    local = jnp.sum(change * change)
    n_dev = lax.axis_size(("mom", "hist"))
    spread = jnp.broadcast_to(local, (n_dev, 1))
    total = jnp.sum(lax.all_to_all(spread, ("mom", "hist"), 0, 0, tiled=True))
    delta = jnp.sqrt(total / (2.0 * K * R * full_hist))
    deltas = deltas.at[ITERS - 1].set(delta)
    green = green + change / (1.0 + delta)
    return (green, deltas)


def solution(mesh):
    placed = (
        P(None, "mom", "hist", None),
        P(None, "mom", None, "hist"),
        P(None, "mom", None, "hist"),
    )
    return jax.shard_map(
        shards,
        mesh=mesh,
        in_specs=placed,
        out_specs=(P(None, "mom", None, "hist"), P()),
        check_vma=False,
    )
```

```python
import math

import jax
import jax.numpy as jnp
from jax import lax
from jax.experimental import pallas as pl
from jax.experimental.pallas import tpu as pltpu
from jax.sharding import PartitionSpec as P

K = 128
R = 4
ITERS = 6


step_size = 0.25
HIGHEST = lax.Precision.HIGHEST


def tables(rows):
    points = jnp.arange(K, dtype=jnp.int32)
    product = rows[:, None] * points[None, :] % K
    phase = product.astype(jnp.float32) * (2.0 * math.pi / K)
    return (jnp.cos(phase), jnp.sin(phase))


def mm(table, field):
    return jnp.dot(table, field, precision=HIGHEST)


def dft(cosine, sine, real, imag):
    both = jnp.concatenate([real, imag], axis=1)
    cr = mm(cosine, both)
    sr = mm(sine, both)
    n = real.shape[1]
    return (cr[:, :n] + sr[:, n:], cr[:, n:] - sr[:, :n])


def gather_rows(block, extra):
    n_mom = lax.axis_size("mom")
    packed = jnp.concatenate([block, jnp.full((8, 128), extra, block.dtype)])
    got = lax.all_to_all(jnp.broadcast_to(packed, (n_mom,) + packed.shape), "mom", 0, 0, tiled=True)
    n = block.shape[0]
    return got[:, :n], jnp.sum(got[:, n, 0])


def to_full_k(rows, lead, k_local, cols):
    g = rows.reshape(rows.shape[0], lead, k_local, R * cols)
    g = jnp.transpose(g, (1, 0, 2, 3))
    return g.reshape(lead, rows.shape[0] * k_local, R * cols)


def hist_reduce(partial, extra, hist_n):
    two, kl, rr, h = partial.shape
    cols = h // hist_n
    x = partial.reshape(two, kl, rr, hist_n, cols)
    x = jnp.transpose(x, (3, 0, 1, 2, 4)).reshape(hist_n, two * kl * rr * cols // 128, 128)
    x = jnp.concatenate([x, jnp.full((hist_n, 8, 128), extra, x.dtype)], axis=1)
    y = lax.all_to_all(x, "hist", 0, 0, tiled=True)
    s = jnp.sum(y, axis=0)
    n = two * kl * rr * cols // 128
    return s[:n].reshape(two, kl, rr, cols), s[n, 0]


def contract_kernel(x_ref, e_ref, p_hbm, o_ref, buf, sem):
    k_local = x_ref.shape[0]
    hist_n = o_ref.shape[0]
    copies = [pltpu.make_async_copy(p_hbm.at[:, k], buf.at[k], sem.at[k]) for k in range(k_local)]
    for c in copies:
        c.start()
    n = 2 * k_local * R
    o_ref[:, n:, :] = jnp.full((hist_n, o_ref.shape[1] - n, 128), e_ref[0], jnp.float32)
    for k in range(k_local):
        copies[k].wait()
        xk = x_ref[k]
        a = jnp.dot(xk, buf[k, 0], precision=HIGHEST, preferred_element_type=jnp.float32)
        b = jnp.dot(xk, buf[k, 1], precision=HIGHEST, preferred_element_type=jnp.float32)
        real = a[:R] - b[R:]
        imag = b[:R] + a[R:]
        for h in range(hist_n):
            o_ref[h, k * R:(k + 1) * R, :] = real[:, h * 128:(h + 1) * 128]
            o_ref[h, n // 2 + k * R:n // 2 + (k + 1) * R, :] = imag[:, h * 128:(h + 1) * 128]


def contract_packed(x, extra, hist_panel, hist_n):
    k_local = x.shape[0]
    rows = 2 * k_local * R + 8
    return pl.pallas_call(
        contract_kernel,
        out_shape=jax.ShapeDtypeStruct((hist_n, rows, 128), jnp.float32),
        in_specs=[
            pl.BlockSpec(memory_space=pltpu.VMEM),
            pl.BlockSpec(memory_space=pltpu.SMEM),
            pl.BlockSpec(memory_space=pl.ANY),
        ],
        out_specs=pl.BlockSpec(memory_space=pltpu.VMEM),
        scratch_shapes=[
            pltpu.VMEM((k_local,) + hist_panel.shape[0:1] + hist_panel.shape[2:], jnp.float32),
            pltpu.SemaphoreType.DMA((k_local,)),
        ],
    )(x, extra.reshape(1), hist_panel)


def hist_reduce_packed(packed, n):
    y = lax.all_to_all(packed, "hist", 0, 0, tiled=True)
    s = jnp.sum(y, axis=0)
    return s[:n], s[n, 0]


def shards(hist_panel, free_rows, screened):
    _, k_local, _, cols = free_rows.shape
    hist_n = hist_panel.shape[3] // cols
    full_hist = hist_panel.shape[3]
    mom_i = lax.axis_index("mom")
    cosine, sine = tables(jnp.arange(K, dtype=jnp.int32))
    own = mom_i * k_local + jnp.arange(k_local, dtype=jnp.int32)
    cos_own, sin_own = tables(own)
    cos_own = cos_own / K
    sin_own = sin_own / K
    nb = 2 * k_local * R * cols

    def sigma_of(full):
        hr, hi = dft(cosine, sine, full[0], full[1])
        pr = hr * screen_hat[0] - hi * screen_hat[1]
        pi = hr * screen_hat[1] + hi * screen_hat[0]
        both = jnp.concatenate([pr, pi], axis=1)
        cb = mm(cos_own, both)
        sb = mm(sin_own, both)
        n = pr.shape[1]
        back_real = cb[:, :n] - sb[:, n:]
        back_imag = cb[:, n:] + sb[:, :n]
        return jnp.stack([-back_imag, back_real]).reshape(2, k_local, R, cols)

    def contract(sigma):
        x = jnp.concatenate([sigma[0], sigma[1]], axis=1)
        a = jnp.einsum("kxs,kst->kxt", x, hist_panel[0], precision=HIGHEST)
        b = jnp.einsum("kxs,kst->kxt", x, hist_panel[1], precision=HIGHEST)
        real = a[:, :R] - b[:, R:]
        imag = b[:, :R] + a[:, R:]
        return jnp.stack([real, imag])

    first = jnp.concatenate([screened.reshape(-1, 128), free_rows.reshape(-1, 128)])
    rows, _ = gather_rows(first, jnp.float32(0.0))
    half = nb // 128
    screen_full = to_full_k(rows[:, :half], 2, k_local, cols)
    green_full = to_full_k(rows[:, half:], 2, k_local, cols)
    screen_hat = dft(cosine, sine, screen_full[0], screen_full[1])

    def integral_of(full, extra):
        sigma = sigma_of(full)
        x = jnp.concatenate([sigma[0], sigma[1]], axis=1)
        packed = contract_packed(x, extra, hist_panel, hist_n)
        got, total = hist_reduce_packed(packed, 2 * k_local * R)
        return got.reshape(2, k_local, R, cols), total

    integral, _ = integral_of(green_full, jnp.float32(0.0))
    def correction(turn, carry):
        green, integral, deltas = carry
        change = free_rows + step_size * integral - green
        local = jnp.sum(change * change)
        rows, mom_sum = gather_rows(change.reshape(-1, 128), local)
        full = to_full_k(rows, 2, k_local, cols)
        step, total = integral_of(full, mom_sum)
        delta = jnp.sqrt(total / (2.0 * K * R * full_hist))
        deltas = lax.dynamic_update_slice(deltas, delta[None], (turn,))
        green = green + change / (1.0 + delta)
        integral = integral + step / (1.0 + delta)
        return (green, integral, deltas)

    carry = (free_rows, integral, jnp.zeros((ITERS,), jnp.float32))
    green, integral, deltas = lax.fori_loop(0, ITERS - 1, correction, carry)
    change = free_rows + step_size * integral - green
    local = jnp.sum(change * change)
    n_dev = lax.axis_size(("mom", "hist"))
    spread = jnp.broadcast_to(local, (n_dev, 1))
    total = jnp.sum(lax.all_to_all(spread, ("mom", "hist"), 0, 0, tiled=True))
    delta = jnp.sqrt(total / (2.0 * K * R * full_hist))
    deltas = deltas.at[ITERS - 1].set(delta)
    green = green + change / (1.0 + delta)
    return (green, deltas)


def solution(mesh):
    placed = (
        P(None, "mom", "hist", None),
        P(None, "mom", None, "hist"),
        P(None, "mom", None, "hist"),
    )
    return jax.shard_map(
        shards,
        mesh=mesh,
        in_specs=placed,
        out_specs=(P(None, "mom", None, "hist"), P()),
        check_vma=False,
    )
```

```python
import math

import jax
import jax.numpy as jnp
from jax import lax
from jax.sharding import PartitionSpec as P

K = 128
R = 4
ITERS = 6


step_size = 0.25
HIGHEST = lax.Precision.HIGHEST


def tables(rows):
    points = jnp.arange(K, dtype=jnp.int32)
    product = rows[:, None] * points[None, :] % K
    phase = product.astype(jnp.float32) * (2.0 * math.pi / K)
    return (jnp.cos(phase), jnp.sin(phase))


def mm(table, field, precision=HIGHEST):
    return jnp.dot(table, field, precision=precision)


def dft(cosine, sine, real, imag, precision=HIGHEST):
    both = jnp.concatenate([real, imag], axis=1)
    out = mm(jnp.concatenate([cosine, sine]), both, precision)
    cr = out[: cosine.shape[0]]
    sr = out[cosine.shape[0]:]
    n = real.shape[1]
    return (cr[:, :n] + sr[:, n:], cr[:, n:] - sr[:, :n])


def gather_rows(block, extra):
    n_mom = lax.axis_size("mom")
    packed = jnp.concatenate([block, jnp.full((8, 128), extra, block.dtype)])
    got = lax.all_to_all(jnp.broadcast_to(packed, (n_mom,) + packed.shape), "mom", 0, 0, tiled=True)
    n = block.shape[0]
    return got[:, :n], jnp.sum(got[:, n, 0])


def to_full_k(rows, lead, k_local, cols):
    g = rows.reshape(rows.shape[0], lead, k_local, R * cols)
    g = jnp.transpose(g, (1, 0, 2, 3))
    return g.reshape(lead, rows.shape[0] * k_local, R * cols)


def hist_reduce(partial, extra, hist_n):
    two, kl, rr, h = partial.shape
    cols = h // hist_n
    x = partial.reshape(two, kl, rr, hist_n, cols)
    x = jnp.transpose(x, (3, 0, 1, 2, 4)).reshape(hist_n, two * kl * rr * cols // 128, 128)
    x = jnp.concatenate([x, jnp.full((hist_n, 8, 128), extra, x.dtype)], axis=1)
    y = lax.all_to_all(x, "hist", 0, 0, tiled=True)
    s = jnp.sum(y, axis=0)
    n = two * kl * rr * cols // 128
    return s[:n].reshape(two, kl, rr, cols), s[n, 0]


def shards(hist_panel, free_rows, screened):
    _, k_local, _, cols = free_rows.shape
    hist_n = hist_panel.shape[3] // cols
    full_hist = hist_panel.shape[3]
    mom_i = lax.axis_index("mom")
    cosine, sine = tables(jnp.arange(K, dtype=jnp.int32))
    own = mom_i * k_local + jnp.arange(k_local, dtype=jnp.int32)
    cos_own, sin_own = tables(own)
    cos_own = cos_own / K
    sin_own = sin_own / K
    nb = 2 * k_local * R * cols

    def sigma_of(full):
        hr, hi = dft(cosine, sine, full[0], full[1], lax.Precision.HIGH)
        pr = hr * screen_hat[0] - hi * screen_hat[1]
        pi = hr * screen_hat[1] + hi * screen_hat[0]
        both = jnp.concatenate([pr, pi], axis=1)
        out = mm(jnp.concatenate([cos_own, sin_own]), both, lax.Precision.HIGH)
        cb = out[:k_local]
        sb = out[k_local:]
        n = pr.shape[1]
        back_real = cb[:, :n] - sb[:, n:]
        back_imag = cb[:, n:] + sb[:, :n]
        return jnp.stack([-back_imag, back_real]).reshape(2, k_local, R, cols)

    def contract(sigma):
        x = jnp.concatenate([sigma[0], sigma[1]], axis=1)
        a = jnp.einsum("kxs,kst->kxt", x, hist_panel[0], precision=HIGHEST)
        b = jnp.einsum("kxs,kst->kxt", x, hist_panel[1], precision=HIGHEST)
        real = a[:, :R] - b[:, R:]
        imag = b[:, :R] + a[:, R:]
        return jnp.stack([real, imag])

    first = jnp.concatenate([screened.reshape(-1, 128), free_rows.reshape(-1, 128)])
    rows, _ = gather_rows(first, jnp.float32(0.0))
    half = nb // 128
    screen_full = to_full_k(rows[:, :half], 2, k_local, cols)
    green_full = to_full_k(rows[:, half:], 2, k_local, cols)
    screen_hat = dft(cosine, sine, screen_full[0], screen_full[1])

    integral, _ = hist_reduce(contract(sigma_of(green_full)), jnp.float32(0.0), hist_n)
    def correction(turn, carry):
        green, integral, deltas = carry
        change = free_rows + step_size * integral - green
        local = jnp.sum(change * change)
        rows, mom_sum = gather_rows(change.reshape(-1, 128), local)
        full = to_full_k(rows, 2, k_local, cols)
        step, total = hist_reduce(contract(sigma_of(full)), mom_sum, hist_n)
        delta = jnp.sqrt(total / (2.0 * K * R * full_hist))
        deltas = lax.dynamic_update_slice(deltas, delta[None], (turn,))
        green = green + change / (1.0 + delta)
        integral = integral + step / (1.0 + delta)
        return (green, integral, deltas)

    carry = (free_rows, integral, jnp.zeros((ITERS,), jnp.float32))
    green, integral, deltas = lax.fori_loop(0, ITERS - 1, correction, carry)
    change = free_rows + step_size * integral - green
    local = jnp.sum(change * change)
    n_dev = lax.axis_size(("mom", "hist"))
    spread = jnp.broadcast_to(local, (n_dev, 1))
    total = jnp.sum(lax.all_to_all(spread, ("mom", "hist"), 0, 0, tiled=True))
    delta = jnp.sqrt(total / (2.0 * K * R * full_hist))
    deltas = deltas.at[ITERS - 1].set(delta)
    green = green + change / (1.0 + delta)
    return (green, deltas)


def solution(mesh):
    placed = (
        P(None, "mom", "hist", None),
        P(None, "mom", None, "hist"),
        P(None, "mom", None, "hist"),
    )
    return jax.shard_map(
        shards,
        mesh=mesh,
        in_specs=placed,
        out_specs=(P(None, "mom", None, "hist"), P()),
        check_vma=False,
    )
```

```python
import math

import jax
import jax.numpy as jnp
from jax import lax
from jax.sharding import PartitionSpec as P

K = 128
R = 4
ITERS = 6


step_size = 0.25
HIGHEST = lax.Precision.HIGHEST


def tables(rows):
    points = jnp.arange(K, dtype=jnp.int32)
    product = rows[:, None] * points[None, :] % K
    phase = product.astype(jnp.float32) * (2.0 * math.pi / K)
    return (jnp.cos(phase), jnp.sin(phase))


def mm(table, field, precision=HIGHEST):
    return jnp.dot(table, field, precision=precision)


def dft(cosine, sine, real, imag, precision=HIGHEST):
    both = jnp.concatenate([real, imag], axis=1)
    out = mm(jnp.concatenate([cosine, sine]), both, precision)
    cr = out[: cosine.shape[0]]
    sr = out[cosine.shape[0]:]
    n = real.shape[1]
    return (cr[:, :n] + sr[:, n:], cr[:, n:] - sr[:, :n])


def gather_rows(block, extra):
    n_mom = lax.axis_size("mom")
    packed = jnp.concatenate([block, jnp.full((8, 128), extra, block.dtype)])
    got = lax.all_to_all(jnp.broadcast_to(packed, (n_mom,) + packed.shape), "mom", 0, 0, tiled=True)
    n = block.shape[0]
    return got[:, :n], jnp.sum(got[:, n, 0])


def to_full_k(rows, lead, k_local, cols):
    g = rows.reshape(rows.shape[0], lead, k_local, R * cols)
    g = jnp.transpose(g, (1, 0, 2, 3))
    return g.reshape(lead, rows.shape[0] * k_local, R * cols)


def hist_reduce(partial, extra, hist_n):
    two, kl, rr, h = partial.shape
    cols = h // hist_n
    x = partial.reshape(two, kl, rr, hist_n, cols)
    x = jnp.transpose(x, (3, 0, 1, 2, 4)).reshape(hist_n, two * kl * rr * cols // 128, 128)
    x = jnp.concatenate([x, jnp.full((hist_n, 8, 128), extra, x.dtype)], axis=1)
    y = lax.all_to_all(x, "hist", 0, 0, tiled=True)
    s = jnp.sum(y, axis=0)
    n = two * kl * rr * cols // 128
    return s[:n].reshape(two, kl, rr, cols), s[n, 0]


def shards(hist_panel, free_rows, screened):
    _, k_local, _, cols = free_rows.shape
    hist_n = hist_panel.shape[3] // cols
    full_hist = hist_panel.shape[3]
    mom_i = lax.axis_index("mom")
    cosine, sine = tables(jnp.arange(K, dtype=jnp.int32))
    own = mom_i * k_local + jnp.arange(k_local, dtype=jnp.int32)
    cos_own, sin_own = tables(own)
    cos_own = cos_own / K
    sin_own = sin_own / K
    nb = 2 * k_local * R * cols

    def sigma_of(full):
        hr, hi = dft(cosine, sine, full[0], full[1], lax.Precision.HIGH)
        pr = hr * screen_hat[0] - hi * screen_hat[1]
        pi = hr * screen_hat[1] + hi * screen_hat[0]
        both = jnp.concatenate([pr, pi], axis=1)
        out = mm(jnp.concatenate([cos_own, sin_own]), both, lax.Precision.HIGH)
        cb = out[:k_local]
        sb = out[k_local:]
        n = pr.shape[1]
        back_real = cb[:, :n] - sb[:, n:]
        back_imag = cb[:, n:] + sb[:, :n]
        return jnp.stack([-back_imag, back_real]).reshape(2, k_local, R, cols)

    def contract(sigma):
        x = jnp.concatenate([sigma[0], sigma[1]], axis=1)
        both = jnp.einsum("kxs,ckst->ckxt", x, hist_panel, precision=HIGHEST)
        a = both[0]
        b = both[1]
        real = a[:, :R] - b[:, R:]
        imag = b[:, :R] + a[:, R:]
        return jnp.stack([real, imag])

    first = jnp.concatenate([screened.reshape(-1, 128), free_rows.reshape(-1, 128)])
    rows, _ = gather_rows(first, jnp.float32(0.0))
    half = nb // 128
    screen_full = to_full_k(rows[:, :half], 2, k_local, cols)
    green_full = to_full_k(rows[:, half:], 2, k_local, cols)
    screen_hat = dft(cosine, sine, screen_full[0], screen_full[1])

    integral, _ = hist_reduce(contract(sigma_of(green_full)), jnp.float32(0.0), hist_n)
    def correction(turn, carry):
        green, integral, deltas = carry
        change = free_rows + step_size * integral - green
        local = jnp.sum(change * change)
        rows, mom_sum = gather_rows(change.reshape(-1, 128), local)
        full = to_full_k(rows, 2, k_local, cols)
        step, total = hist_reduce(contract(sigma_of(full)), mom_sum, hist_n)
        delta = jnp.sqrt(total / (2.0 * K * R * full_hist))
        deltas = lax.dynamic_update_slice(deltas, delta[None], (turn,))
        green = green + change / (1.0 + delta)
        integral = integral + step / (1.0 + delta)
        return (green, integral, deltas)

    carry = (free_rows, integral, jnp.zeros((ITERS,), jnp.float32))
    green, integral, deltas = lax.fori_loop(0, ITERS - 1, correction, carry)
    change = free_rows + step_size * integral - green
    local = jnp.sum(change * change)
    n_dev = lax.axis_size(("mom", "hist"))
    spread = jnp.broadcast_to(local, (n_dev, 1))
    total = jnp.sum(lax.all_to_all(spread, ("mom", "hist"), 0, 0, tiled=True))
    delta = jnp.sqrt(total / (2.0 * K * R * full_hist))
    deltas = deltas.at[ITERS - 1].set(delta)
    green = green + change / (1.0 + delta)
    return (green, deltas)


def solution(mesh):
    placed = (
        P(None, "mom", "hist", None),
        P(None, "mom", None, "hist"),
        P(None, "mom", None, "hist"),
    )
    return jax.shard_map(
        shards,
        mesh=mesh,
        in_specs=placed,
        out_specs=(P(None, "mom", None, "hist"), P()),
        check_vma=False,
    )
```

```python
import math

import jax
import jax.numpy as jnp
from jax import lax
from jax.sharding import PartitionSpec as P

K = 128
R = 4
ITERS = 6


step_size = 0.25
HIGHEST = lax.Precision.HIGHEST


def tables(rows):
    points = jnp.arange(K, dtype=jnp.int32)
    product = rows[:, None] * points[None, :] % K
    phase = product.astype(jnp.float32) * (2.0 * math.pi / K)
    return (jnp.cos(phase), jnp.sin(phase))


def mm(table, field, precision=HIGHEST):
    return jnp.dot(table, field, precision=precision)


def dft(cosine, sine, real, imag, precision=HIGHEST):
    both = jnp.concatenate([real, imag], axis=1)
    out = mm(jnp.concatenate([cosine, sine]), both, precision)
    cr = out[: cosine.shape[0]]
    sr = out[cosine.shape[0]:]
    n = real.shape[1]
    return (cr[:, :n] + sr[:, n:], cr[:, n:] - sr[:, :n])


def gather_rows(block, extra):
    n_mom = lax.axis_size("mom")
    packed = jnp.concatenate([block, jnp.full((8, 128), extra, block.dtype)])
    got = lax.all_to_all(jnp.broadcast_to(packed, (n_mom,) + packed.shape), "mom", 0, 0, tiled=True)
    n = block.shape[0]
    return got[:, :n], got[:, n, 0]


def to_full_k(rows, lead, k_local, cols):
    g = rows.reshape(rows.shape[0], lead, k_local, R * cols)
    g = jnp.transpose(g, (1, 0, 2, 3))
    return g.reshape(lead, rows.shape[0] * k_local, R * cols)


def hist_reduce(partial, extra, hist_n):
    two, kl, rr, h = partial.shape
    cols = h // hist_n
    x = partial.reshape(two, kl, rr, hist_n, cols)
    x = jnp.transpose(x, (3, 0, 1, 2, 4)).reshape(hist_n, two * kl * rr * cols // 128, 128)
    tile = jnp.pad(extra[None, :], ((0, 7), (0, 128 - extra.shape[0])))
    x = jnp.concatenate([x, jnp.broadcast_to(tile, (hist_n, 8, 128))], axis=1)
    y = lax.all_to_all(x, "hist", 0, 0, tiled=True)
    n = two * kl * rr * cols // 128
    total = jnp.sum(jnp.sum(y[:, n, : extra.shape[0]], axis=0))
    return jnp.sum(y[:, :n], axis=0).reshape(two, kl, rr, cols), total


def shards(hist_panel, free_rows, screened):
    _, k_local, _, cols = free_rows.shape
    hist_n = hist_panel.shape[3] // cols
    full_hist = hist_panel.shape[3]
    mom_i = lax.axis_index("mom")
    cosine, sine = tables(jnp.arange(K, dtype=jnp.int32))
    own = mom_i * k_local + jnp.arange(k_local, dtype=jnp.int32)
    cos_own, sin_own = tables(own)
    cos_own = cos_own / K
    sin_own = sin_own / K
    nb = 2 * k_local * R * cols

    def sigma_of(full):
        hr, hi = dft(cosine, sine, full[0], full[1], lax.Precision.HIGH)
        pr = hr * screen_hat[0] - hi * screen_hat[1]
        pi = hr * screen_hat[1] + hi * screen_hat[0]
        both = jnp.concatenate([pr, pi], axis=1)
        out = mm(jnp.concatenate([cos_own, sin_own]), both, lax.Precision.HIGH)
        cb = out[:k_local]
        sb = out[k_local:]
        n = pr.shape[1]
        back_real = cb[:, :n] - sb[:, n:]
        back_imag = cb[:, n:] + sb[:, :n]
        return jnp.stack([-back_imag, back_real]).reshape(2, k_local, R, cols)

    def contract(sigma):
        x = jnp.concatenate([sigma[0], sigma[1]], axis=1)
        a = jnp.einsum("kxs,kst->kxt", x, hist_panel[0], precision=HIGHEST)
        b = jnp.einsum("kxs,kst->kxt", x, hist_panel[1], precision=HIGHEST)
        real = a[:, :R] - b[:, R:]
        imag = b[:, :R] + a[:, R:]
        return jnp.stack([real, imag])

    first = jnp.concatenate([screened.reshape(-1, 128), free_rows.reshape(-1, 128)])
    rows, _ = gather_rows(first, jnp.float32(0.0))
    half = nb // 128
    screen_full = to_full_k(rows[:, :half], 2, k_local, cols)
    green_full = to_full_k(rows[:, half:], 2, k_local, cols)
    screen_hat = dft(cosine, sine, screen_full[0], screen_full[1])

    integral, _ = hist_reduce(contract(sigma_of(green_full)), jnp.zeros((lax.axis_size("mom"),), jnp.float32), hist_n)
    def correction(turn, carry):
        green, integral, deltas = carry
        change = free_rows + step_size * integral - green
        local = jnp.sum(change * change)
        rows, mom_sum = gather_rows(change.reshape(-1, 128), local)
        full = to_full_k(rows, 2, k_local, cols)
        step, total = hist_reduce(contract(sigma_of(full)), mom_sum, hist_n)
        delta = jnp.sqrt(total / (2.0 * K * R * full_hist))
        deltas = lax.dynamic_update_slice(deltas, delta[None], (turn,))
        green = green + change / (1.0 + delta)
        integral = integral + step / (1.0 + delta)
        return (green, integral, deltas)

    carry = (free_rows, integral, jnp.zeros((ITERS,), jnp.float32))
    green, integral, deltas = lax.fori_loop(0, ITERS - 1, correction, carry)
    change = free_rows + step_size * integral - green
    local = jnp.sum(change * change)
    n_dev = lax.axis_size(("mom", "hist"))
    spread = jnp.broadcast_to(local, (n_dev, 1))
    total = jnp.sum(lax.all_to_all(spread, ("mom", "hist"), 0, 0, tiled=True))
    delta = jnp.sqrt(total / (2.0 * K * R * full_hist))
    deltas = deltas.at[ITERS - 1].set(delta)
    green = green + change / (1.0 + delta)
    return (green, deltas)


def solution(mesh):
    placed = (
        P(None, "mom", "hist", None),
        P(None, "mom", None, "hist"),
        P(None, "mom", None, "hist"),
    )
    return jax.shard_map(
        shards,
        mesh=mesh,
        in_specs=placed,
        out_specs=(P(None, "mom", None, "hist"), P()),
        check_vma=False,
    )
```

```python
import math

import jax
import jax.numpy as jnp
from jax import lax
from jax.sharding import PartitionSpec as P

K = 128
R = 4
ITERS = 6


step_size = 0.25
HIGHEST = lax.Precision.HIGHEST


def tables(rows):
    points = jnp.arange(K, dtype=jnp.int32)
    product = rows[:, None] * points[None, :] % K
    phase = product.astype(jnp.float32) * (2.0 * math.pi / K)
    return (jnp.cos(phase), jnp.sin(phase))


def mm(table, field, precision=HIGHEST):
    return jnp.dot(table, field, precision=precision)


def dft(cosine, sine, real, imag, precision=HIGHEST):
    both = jnp.concatenate([real, imag], axis=1)
    out = mm(jnp.concatenate([cosine, sine]), both, precision)
    cr = out[: cosine.shape[0]]
    sr = out[cosine.shape[0]:]
    n = real.shape[1]
    return (cr[:, :n] + sr[:, n:], cr[:, n:] - sr[:, :n])


def gather_rows(block):
    n_mom = lax.axis_size("mom")
    return lax.all_to_all(jnp.broadcast_to(block, (n_mom,) + block.shape), "mom", 0, 0, tiled=True)


def to_full_k(rows, lead, k_local, cols):
    g = rows.reshape(rows.shape[0], lead, k_local, R * cols)
    g = jnp.transpose(g, (1, 0, 2, 3))
    return g.reshape(lead, rows.shape[0] * k_local, R * cols)


def hist_reduce(partial, extra, hist_n):
    two, kl, rr, h = partial.shape
    cols = h // hist_n
    x = partial.reshape(two, kl, rr, hist_n, cols)
    x = jnp.transpose(x, (3, 0, 1, 2, 4)).reshape(hist_n, two * kl * rr * cols // 128, 128)
    tile = jnp.pad(extra[None, :], ((0, 7), (0, 128 - extra.shape[0])))
    x = jnp.concatenate([x, jnp.broadcast_to(tile, (hist_n, 8, 128))], axis=1)
    y = lax.all_to_all(x, "hist", 0, 0, tiled=True)
    n = two * kl * rr * cols // 128
    total = jnp.sum(jnp.sum(y[:, n, : extra.shape[0]], axis=0))
    return jnp.sum(y[:, :n], axis=0).reshape(two, kl, rr, cols), total


def shards(hist_panel, free_rows, screened):
    _, k_local, _, cols = free_rows.shape
    hist_n = hist_panel.shape[3] // cols
    full_hist = hist_panel.shape[3]
    mom_i = lax.axis_index("mom")
    cosine, sine = tables(jnp.arange(K, dtype=jnp.int32))
    own = mom_i * k_local + jnp.arange(k_local, dtype=jnp.int32)
    cos_own, sin_own = tables(own)
    cos_own = cos_own / K
    sin_own = sin_own / K
    nb = 2 * k_local * R * cols

    def sigma_of(full):
        hr, hi = dft(cosine, sine, full[0], full[1], lax.Precision.HIGH)
        pr = hr * screen_hat[0] - hi * screen_hat[1]
        pi = hr * screen_hat[1] + hi * screen_hat[0]
        both = jnp.concatenate([pr, pi], axis=1)
        out = mm(jnp.concatenate([cos_own, sin_own]), both, lax.Precision.HIGH)
        cb = out[:k_local]
        sb = out[k_local:]
        n = pr.shape[1]
        back_real = cb[:, :n] - sb[:, n:]
        back_imag = cb[:, n:] + sb[:, :n]
        return jnp.stack([-back_imag, back_real]).reshape(2, k_local, R, cols)

    def contract(sigma):
        x = jnp.concatenate([sigma[0], sigma[1]], axis=1)
        a = jnp.einsum("kxs,kst->kxt", x, hist_panel[0], precision=HIGHEST)
        b = jnp.einsum("kxs,kst->kxt", x, hist_panel[1], precision=HIGHEST)
        real = a[:, :R] - b[:, R:]
        imag = b[:, :R] + a[:, R:]
        return jnp.stack([real, imag])

    first = jnp.concatenate([screened.reshape(-1, 128), free_rows.reshape(-1, 128)])
    rows = gather_rows(first)
    half = nb // 128
    screen_full = to_full_k(rows[:, :half], 2, k_local, cols)
    green_full = to_full_k(rows[:, half:], 2, k_local, cols)
    screen_hat = dft(cosine, sine, screen_full[0], screen_full[1])

    integral, _ = hist_reduce(contract(sigma_of(green_full)), jnp.zeros((lax.axis_size("mom"),), jnp.float32), hist_n)
    def correction(turn, carry):
        green, integral, deltas = carry
        change = free_rows + step_size * integral - green
        rows = gather_rows(change.reshape(-1, 128))
        mom_sums = jnp.sum(rows * rows, axis=(1, 2))
        full = to_full_k(rows, 2, k_local, cols)
        step, total = hist_reduce(contract(sigma_of(full)), mom_sums, hist_n)
        delta = jnp.sqrt(total / (2.0 * K * R * full_hist))
        deltas = lax.dynamic_update_slice(deltas, delta[None], (turn,))
        green = green + change / (1.0 + delta)
        integral = integral + step / (1.0 + delta)
        return (green, integral, deltas)

    carry = (free_rows, integral, jnp.zeros((ITERS,), jnp.float32))
    green, integral, deltas = lax.fori_loop(0, ITERS - 1, correction, carry)
    change = free_rows + step_size * integral - green
    local = jnp.sum(change * change)
    n_dev = lax.axis_size(("mom", "hist"))
    spread = jnp.broadcast_to(local, (n_dev, 1))
    total = jnp.sum(lax.all_to_all(spread, ("mom", "hist"), 0, 0, tiled=True))
    delta = jnp.sqrt(total / (2.0 * K * R * full_hist))
    deltas = deltas.at[ITERS - 1].set(delta)
    green = green + change / (1.0 + delta)
    return (green, deltas)


def solution(mesh):
    placed = (
        P(None, "mom", "hist", None),
        P(None, "mom", None, "hist"),
        P(None, "mom", None, "hist"),
    )
    return jax.shard_map(
        shards,
        mesh=mesh,
        in_specs=placed,
        out_specs=(P(None, "mom", None, "hist"), P()),
        check_vma=False,
    )
```

```python
import math

import jax
import jax.numpy as jnp
from jax import lax
from jax.sharding import PartitionSpec as P

K = 128
R = 4
ITERS = 6


step_size = 0.25
HIGHEST = lax.Precision.HIGHEST


def tables(rows):
    points = jnp.arange(K, dtype=jnp.int32)
    product = rows[:, None] * points[None, :] % K
    phase = product.astype(jnp.float32) * (2.0 * math.pi / K)
    return (jnp.cos(phase), jnp.sin(phase))


def mm(table, field, precision=HIGHEST):
    return jnp.dot(table, field, precision=precision)


def dft(cosine, sine, real, imag, precision=HIGHEST):
    both = jnp.concatenate([real, imag], axis=1)
    out = mm(jnp.concatenate([cosine, sine]), both, precision)
    cr = out[: cosine.shape[0]]
    sr = out[cosine.shape[0]:]
    n = real.shape[1]
    return (cr[:, :n] + sr[:, n:], cr[:, n:] - sr[:, :n])


def gather_rows(block):
    n_mom = lax.axis_size("mom")
    return lax.all_to_all(jnp.broadcast_to(block, (n_mom,) + block.shape), "mom", 0, 0, tiled=True)


def to_full_k(rows, lead, k_local, cols):
    g = rows.reshape(rows.shape[0], lead, k_local, R * cols)
    g = jnp.transpose(g, (1, 0, 2, 3))
    return g.reshape(lead, rows.shape[0] * k_local, R * cols)


def hist_reduce(partial, extra, hist_n):
    two, kl, rr, h = partial.shape
    cols = h // hist_n
    x = partial.reshape(two, kl, rr, hist_n, cols)
    x = jnp.transpose(x, (3, 0, 1, 2, 4)).reshape(hist_n, two * kl * rr * cols // 128, 128)
    tile = jnp.pad(extra[None, :], ((0, 7), (0, 128 - extra.shape[0])))
    x = jnp.concatenate([x, jnp.broadcast_to(tile, (hist_n, 8, 128))], axis=1)
    y = lax.all_to_all(x, "hist", 0, 0, tiled=True)
    n = two * kl * rr * cols // 128
    total = jnp.sum(jnp.sum(y[:, n, : extra.shape[0]], axis=0))
    return jnp.sum(y[:, :n], axis=0).reshape(two, kl, rr, cols), total


def shards(hist_panel, free_rows, screened):
    _, k_local, _, cols = free_rows.shape
    hist_n = hist_panel.shape[3] // cols
    full_hist = hist_panel.shape[3]
    mom_i = lax.axis_index("mom")
    cosine, sine = tables(jnp.arange(K, dtype=jnp.int32))
    own = mom_i * k_local + jnp.arange(k_local, dtype=jnp.int32)
    cos_own, sin_own = tables(own)
    cos_own = cos_own / K
    sin_own = sin_own / K
    nb = 2 * k_local * R * cols

    def sigma_of(full, precision=lax.Precision.HIGH):
        hr, hi = dft(cosine, sine, full[0], full[1], precision)
        pr = hr * screen_hat[0] - hi * screen_hat[1]
        pi = hr * screen_hat[1] + hi * screen_hat[0]
        both = jnp.concatenate([pr, pi], axis=1)
        out = mm(jnp.concatenate([cos_own, sin_own]), both, precision)
        cb = out[:k_local]
        sb = out[k_local:]
        n = pr.shape[1]
        back_real = cb[:, :n] - sb[:, n:]
        back_imag = cb[:, n:] + sb[:, :n]
        return jnp.stack([-back_imag, back_real]).reshape(2, k_local, R, cols)

    def contract(sigma):
        x = jnp.concatenate([sigma[0], sigma[1]], axis=1)
        a = jnp.einsum("kxs,kst->kxt", x, hist_panel[0], precision=HIGHEST)
        b = jnp.einsum("kxs,kst->kxt", x, hist_panel[1], precision=HIGHEST)
        real = a[:, :R] - b[:, R:]
        imag = b[:, :R] + a[:, R:]
        return jnp.stack([real, imag])

    first = jnp.concatenate([screened.reshape(-1, 128), free_rows.reshape(-1, 128)])
    rows = gather_rows(first)
    half = nb // 128
    screen_full = to_full_k(rows[:, :half], 2, k_local, cols)
    green_full = to_full_k(rows[:, half:], 2, k_local, cols)
    screen_hat = dft(cosine, sine, screen_full[0], screen_full[1])

    integral, _ = hist_reduce(contract(sigma_of(green_full, HIGHEST)), jnp.zeros((lax.axis_size("mom"),), jnp.float32), hist_n)
    def correction(turn, carry):
        green, integral, deltas = carry
        change = free_rows + step_size * integral - green
        rows = gather_rows(change.reshape(-1, 128))
        mom_sums = jnp.sum(rows * rows, axis=(1, 2))
        full = to_full_k(rows, 2, k_local, cols)
        step, total = hist_reduce(contract(sigma_of(full)), mom_sums, hist_n)
        delta = jnp.sqrt(total / (2.0 * K * R * full_hist))
        deltas = lax.dynamic_update_slice(deltas, delta[None], (turn,))
        green = green + change / (1.0 + delta)
        integral = integral + step / (1.0 + delta)
        return (green, integral, deltas)

    carry = (free_rows, integral, jnp.zeros((ITERS,), jnp.float32))
    green, integral, deltas = lax.fori_loop(0, ITERS - 1, correction, carry)
    change = free_rows + step_size * integral - green
    local = jnp.sum(change * change)
    n_dev = lax.axis_size(("mom", "hist"))
    spread = jnp.broadcast_to(local, (n_dev, 1))
    total = jnp.sum(lax.all_to_all(spread, ("mom", "hist"), 0, 0, tiled=True))
    delta = jnp.sqrt(total / (2.0 * K * R * full_hist))
    deltas = deltas.at[ITERS - 1].set(delta)
    green = green + change / (1.0 + delta)
    return (green, deltas)


def solution(mesh):
    placed = (
        P(None, "mom", "hist", None),
        P(None, "mom", None, "hist"),
        P(None, "mom", None, "hist"),
    )
    return jax.shard_map(
        shards,
        mesh=mesh,
        in_specs=placed,
        out_specs=(P(None, "mom", None, "hist"), P()),
        check_vma=False,
    )
```

```python
import math

import jax
import jax.numpy as jnp
from jax import lax
from jax.sharding import PartitionSpec as P

K = 128
R = 4
ITERS = 6


step_size = 0.25
HIGHEST = lax.Precision.HIGHEST


def tables(rows):
    points = jnp.arange(K, dtype=jnp.int32)
    product = rows[:, None] * points[None, :] % K
    phase = product.astype(jnp.float32) * (2.0 * math.pi / K)
    return (jnp.cos(phase), jnp.sin(phase))


def mm(table, field, precision=HIGHEST):
    return jnp.dot(table, field, precision=precision)


def dft(cosine, sine, real, imag, precision=HIGHEST):
    both = jnp.concatenate([real, imag], axis=1)
    out = mm(jnp.concatenate([cosine, sine]), both, precision)
    cr = out[: cosine.shape[0]]
    sr = out[cosine.shape[0]:]
    n = real.shape[1]
    return (cr[:, :n] + sr[:, n:], cr[:, n:] - sr[:, :n])


def gather_rows(block):
    n_mom = lax.axis_size("mom")
    return lax.all_to_all(jnp.broadcast_to(block, (n_mom,) + block.shape), "mom", 0, 0, tiled=True)


def to_full_k(rows, lead, k_local, cols):
    g = rows.reshape(rows.shape[0], lead, k_local, R * cols)
    g = jnp.transpose(g, (1, 0, 2, 3))
    return g.reshape(lead, rows.shape[0] * k_local, R * cols)


def hist_reduce(partial, extra, hist_n):
    _, two, kl, rr, cols = partial.shape
    x = partial.reshape(hist_n, two * kl * rr * cols // 128, 128)
    tile = jnp.pad(extra[None, :], ((0, 7), (0, 128 - extra.shape[0])))
    x = jnp.concatenate([x, jnp.broadcast_to(tile, (hist_n, 8, 128))], axis=1)
    y = lax.all_to_all(x, "hist", 0, 0, tiled=True)
    n = two * kl * rr * cols // 128
    total = jnp.sum(jnp.sum(y[:, n, : extra.shape[0]], axis=0))
    return jnp.sum(y[:, :n], axis=0).reshape(two, kl, rr, cols), total


def shards(hist_panel, free_rows, screened):
    _, k_local, _, cols = free_rows.shape
    hist_n = hist_panel.shape[3] // cols
    full_hist = hist_panel.shape[3]
    mom_i = lax.axis_index("mom")
    cosine, sine = tables(jnp.arange(K, dtype=jnp.int32))
    own = mom_i * k_local + jnp.arange(k_local, dtype=jnp.int32)
    cos_own, sin_own = tables(own)
    cos_own = cos_own / K
    sin_own = sin_own / K
    nb = 2 * k_local * R * cols

    def sigma_of(full, precision=lax.Precision.HIGH):
        hr, hi = dft(cosine, sine, full[0], full[1], precision)
        pr = hr * screen_hat[0] - hi * screen_hat[1]
        pi = hr * screen_hat[1] + hi * screen_hat[0]
        both = jnp.concatenate([pr, pi], axis=1)
        out = mm(jnp.concatenate([cos_own, sin_own]), both, precision)
        cb = out[:k_local]
        sb = out[k_local:]
        n = pr.shape[1]
        back_real = cb[:, :n] - sb[:, n:]
        back_imag = cb[:, n:] + sb[:, :n]
        return jnp.stack([-back_imag, back_real]).reshape(2, k_local, R, cols)

    def contract(sigma):
        x = jnp.concatenate([sigma[0], sigma[1]], axis=1)
        panel = hist_panel.reshape(hist_panel.shape[:3] + (hist_n, cols))
        a = jnp.einsum("kxs,kshu->hkxu", x, panel[0], precision=HIGHEST)
        b = jnp.einsum("kxs,kshu->hkxu", x, panel[1], precision=HIGHEST)
        real = a[:, :, :R] - b[:, :, R:]
        imag = b[:, :, :R] + a[:, :, R:]
        return jnp.stack([real, imag], axis=1)

    first = jnp.concatenate([screened.reshape(-1, 128), free_rows.reshape(-1, 128)])
    rows = gather_rows(first)
    half = nb // 128
    screen_full = to_full_k(rows[:, :half], 2, k_local, cols)
    green_full = to_full_k(rows[:, half:], 2, k_local, cols)
    screen_hat = dft(cosine, sine, screen_full[0], screen_full[1])

    integral, _ = hist_reduce(contract(sigma_of(green_full, HIGHEST)), jnp.zeros((lax.axis_size("mom"),), jnp.float32), hist_n)
    def correction(turn, carry):
        green, integral, deltas = carry
        change = free_rows + step_size * integral - green
        rows = gather_rows(change.reshape(-1, 128))
        mom_sums = jnp.sum(rows * rows, axis=(1, 2))
        full = to_full_k(rows, 2, k_local, cols)
        step, total = hist_reduce(contract(sigma_of(full)), mom_sums, hist_n)
        delta = jnp.sqrt(total / (2.0 * K * R * full_hist))
        deltas = lax.dynamic_update_slice(deltas, delta[None], (turn,))
        green = green + change / (1.0 + delta)
        integral = integral + step / (1.0 + delta)
        return (green, integral, deltas)

    carry = (free_rows, integral, jnp.zeros((ITERS,), jnp.float32))
    green, integral, deltas = lax.fori_loop(0, ITERS - 1, correction, carry)
    change = free_rows + step_size * integral - green
    local = jnp.sum(change * change)
    n_dev = lax.axis_size(("mom", "hist"))
    spread = jnp.broadcast_to(local, (n_dev, 1))
    total = jnp.sum(lax.all_to_all(spread, ("mom", "hist"), 0, 0, tiled=True))
    delta = jnp.sqrt(total / (2.0 * K * R * full_hist))
    deltas = deltas.at[ITERS - 1].set(delta)
    green = green + change / (1.0 + delta)
    return (green, deltas)


def solution(mesh):
    placed = (
        P(None, "mom", "hist", None),
        P(None, "mom", None, "hist"),
        P(None, "mom", None, "hist"),
    )
    return jax.shard_map(
        shards,
        mesh=mesh,
        in_specs=placed,
        out_specs=(P(None, "mom", None, "hist"), P()),
        check_vma=False,
    )
```

```python
import math

import jax
import jax.numpy as jnp
from jax import lax
from jax.sharding import PartitionSpec as P

K = 128
R = 4
ITERS = 6


step_size = 0.25
HIGHEST = lax.Precision.HIGHEST


def tables(rows):
    points = jnp.arange(K, dtype=jnp.int32)
    product = rows[:, None] * points[None, :] % K
    phase = product.astype(jnp.float32) * (2.0 * math.pi / K)
    return (jnp.cos(phase), jnp.sin(phase))


def mm(table, field, precision=HIGHEST):
    return jnp.dot(table, field, precision=precision)


def dft(cosine, sine, real, imag, precision=HIGHEST):
    both = jnp.concatenate([real, imag], axis=1)
    out = mm(jnp.concatenate([cosine, sine]), both, precision)
    cr = out[: cosine.shape[0]]
    sr = out[cosine.shape[0]:]
    n = real.shape[1]
    return (cr[:, :n] + sr[:, n:], cr[:, n:] - sr[:, :n])


def gather_rows(block):
    n_mom = lax.axis_size("mom")
    return lax.all_to_all(jnp.broadcast_to(block, (n_mom,) + block.shape), "mom", 0, 0, tiled=True)


def to_full_k(rows, lead, k_local, cols):
    g = rows.reshape(rows.shape[0], lead, k_local, R * cols)
    g = jnp.transpose(g, (1, 0, 2, 3))
    return g.reshape(lead, rows.shape[0] * k_local, R * cols)


def hist_reduce(partial, extra, hist_n):
    two, kl, rr, h = partial.shape
    cols = h // hist_n
    x = partial.reshape(two, kl, rr, hist_n, cols)
    x = jnp.transpose(x, (3, 0, 1, 2, 4)).reshape(hist_n, two * kl * rr * cols // 128, 128)
    tile = jnp.pad(extra[None, :], ((0, 7), (0, 128 - extra.shape[0])))
    x = jnp.concatenate([x, jnp.broadcast_to(tile, (hist_n, 8, 128))], axis=1)
    y = lax.all_to_all(x, "hist", 0, 0, tiled=True)
    n = two * kl * rr * cols // 128
    total = jnp.sum(jnp.sum(y[:, n, : extra.shape[0]], axis=0))
    return jnp.sum(y[:, :n], axis=0).reshape(two, kl, rr, cols), total


def shards(hist_panel, free_rows, screened):
    _, k_local, _, cols = free_rows.shape
    hist_n = hist_panel.shape[3] // cols
    full_hist = hist_panel.shape[3]
    mom_i = lax.axis_index("mom")
    cosine, sine = tables(jnp.arange(K, dtype=jnp.int32))
    own = mom_i * k_local + jnp.arange(k_local, dtype=jnp.int32)
    cos_own, sin_own = tables(own)
    cos_own = cos_own / K
    sin_own = sin_own / K
    nb = 2 * k_local * R * cols

    def sigma_of(full, precision=lax.Precision.HIGH):
        hr, hi = dft(cosine, sine, full[0], full[1], precision)
        pr = hr * screen_hat[0] - hi * screen_hat[1]
        pi = hr * screen_hat[1] + hi * screen_hat[0]
        both = jnp.concatenate([pr, pi], axis=1)
        out = mm(jnp.concatenate([cos_own, sin_own]), both, precision)
        cb = out[:k_local]
        sb = out[k_local:]
        n = pr.shape[1]
        back_real = cb[:, :n] - sb[:, n:]
        back_imag = cb[:, n:] + sb[:, :n]
        return jnp.stack([-back_imag, back_real]).reshape(2, k_local, R, cols)

    def contract(sigma, precision=lax.Precision.HIGH):
        x = jnp.concatenate([sigma[0], sigma[1]], axis=1)
        a = jnp.einsum("kxs,kst->kxt", x, hist_panel[0], precision=precision)
        b = jnp.einsum("kxs,kst->kxt", x, hist_panel[1], precision=precision)
        real = a[:, :R] - b[:, R:]
        imag = b[:, :R] + a[:, R:]
        return jnp.stack([real, imag])

    first = jnp.concatenate([screened.reshape(-1, 128), free_rows.reshape(-1, 128)])
    rows = gather_rows(first)
    half = nb // 128
    screen_full = to_full_k(rows[:, :half], 2, k_local, cols)
    green_full = to_full_k(rows[:, half:], 2, k_local, cols)
    screen_hat = dft(cosine, sine, screen_full[0], screen_full[1])

    integral, _ = hist_reduce(contract(sigma_of(green_full, HIGHEST), HIGHEST), jnp.zeros((lax.axis_size("mom"),), jnp.float32), hist_n)
    def correction(turn, carry):
        green, integral, deltas = carry
        change = free_rows + step_size * integral - green
        rows = gather_rows(change.reshape(-1, 128))
        mom_sums = jnp.sum(rows * rows, axis=(1, 2))
        full = to_full_k(rows, 2, k_local, cols)
        step, total = hist_reduce(contract(sigma_of(full)), mom_sums, hist_n)
        delta = jnp.sqrt(total / (2.0 * K * R * full_hist))
        deltas = lax.dynamic_update_slice(deltas, delta[None], (turn,))
        green = green + change / (1.0 + delta)
        integral = integral + step / (1.0 + delta)
        return (green, integral, deltas)

    carry = (free_rows, integral, jnp.zeros((ITERS,), jnp.float32))
    green, integral, deltas = lax.fori_loop(0, ITERS - 1, correction, carry)
    change = free_rows + step_size * integral - green
    local = jnp.sum(change * change)
    n_dev = lax.axis_size(("mom", "hist"))
    spread = jnp.broadcast_to(local, (n_dev, 1))
    total = jnp.sum(lax.all_to_all(spread, ("mom", "hist"), 0, 0, tiled=True))
    delta = jnp.sqrt(total / (2.0 * K * R * full_hist))
    deltas = deltas.at[ITERS - 1].set(delta)
    green = green + change / (1.0 + delta)
    return (green, deltas)


def solution(mesh):
    placed = (
        P(None, "mom", "hist", None),
        P(None, "mom", None, "hist"),
        P(None, "mom", None, "hist"),
    )
    return jax.shard_map(
        shards,
        mesh=mesh,
        in_specs=placed,
        out_specs=(P(None, "mom", None, "hist"), P()),
        check_vma=False,
    )
```

```python
import math

import jax
import jax.numpy as jnp
from jax import lax
from jax.sharding import PartitionSpec as P

K = 128
R = 4
ITERS = 6


step_size = 0.25
HIGHEST = lax.Precision.HIGHEST


def tables(rows):
    points = jnp.arange(K, dtype=jnp.int32)
    product = rows[:, None] * points[None, :] % K
    phase = product.astype(jnp.float32) * (2.0 * math.pi / K)
    return (jnp.cos(phase), jnp.sin(phase))


def mm(table, field, precision=HIGHEST):
    return jnp.dot(table, field, precision=precision)


def dft(cosine, sine, real, imag, precision=HIGHEST):
    both = jnp.concatenate([real, imag], axis=1)
    out = mm(jnp.concatenate([cosine, sine]), both, precision)
    cr = out[: cosine.shape[0]]
    sr = out[cosine.shape[0]:]
    n = real.shape[1]
    return (cr[:, :n] + sr[:, n:], cr[:, n:] - sr[:, :n])


def gather_rows(block):
    n_mom = lax.axis_size("mom")
    return lax.all_to_all(jnp.broadcast_to(block, (n_mom,) + block.shape), "mom", 0, 0, tiled=True)


def to_full_k(rows, lead, k_local, cols):
    g = rows.reshape(rows.shape[0], lead, k_local, R * cols)
    g = jnp.transpose(g, (1, 0, 2, 3))
    return g.reshape(lead, rows.shape[0] * k_local, R * cols)


def hist_reduce(partial, extra, hist_n):
    two, kl, rr, h = partial.shape
    cols = h // hist_n
    x = partial.reshape(two, kl, rr, hist_n, cols)
    x = jnp.transpose(x, (3, 0, 1, 2, 4)).reshape(hist_n, two * kl * rr * cols // 128, 128)
    tile = jnp.pad(extra[None, :], ((0, 7), (0, 128 - extra.shape[0])))
    x = jnp.concatenate([x, jnp.broadcast_to(tile, (hist_n, 8, 128))], axis=1)
    y = lax.all_to_all(x, "hist", 0, 0, tiled=True)
    n = two * kl * rr * cols // 128
    total = jnp.sum(jnp.sum(y[:, n, : extra.shape[0]], axis=0))
    return jnp.sum(y[:, :n], axis=0).reshape(two, kl, rr, cols), total


def shards(hist_panel, free_rows, screened):
    _, k_local, _, cols = free_rows.shape
    hist_n = hist_panel.shape[3] // cols
    full_hist = hist_panel.shape[3]
    mom_i = lax.axis_index("mom")
    cosine, sine = tables(jnp.arange(K, dtype=jnp.int32))
    own = mom_i * k_local + jnp.arange(k_local, dtype=jnp.int32)
    cos_own, sin_own = tables(own)
    cos_own = cos_own / K
    sin_own = sin_own / K
    nb = 2 * k_local * R * cols

    def sigma_of(full, precision=lax.Precision.HIGH):
        hr, hi = dft(cosine, sine, full[0], full[1], precision)
        pr = hr * screen_hat[0] - hi * screen_hat[1]
        pi = hr * screen_hat[1] + hi * screen_hat[0]
        both = jnp.concatenate([pr, pi], axis=1)
        out = mm(jnp.concatenate([cos_own, sin_own]), both, precision)
        cb = out[:k_local]
        sb = out[k_local:]
        n = pr.shape[1]
        back_real = cb[:, :n] - sb[:, n:]
        back_imag = cb[:, n:] + sb[:, :n]
        return jnp.stack([-back_imag, back_real]).reshape(2, k_local, R, cols)

    def contract(sigma, precision=lax.Precision.HIGH):
        x = jnp.concatenate([sigma[0], sigma[1]], axis=1)
        a = jnp.einsum("kxs,kst->kxt", x, hist_panel[0], precision=precision)
        b = jnp.einsum("kxs,kst->kxt", x, hist_panel[1], precision=precision)
        real = a[:, :R] - b[:, R:]
        imag = b[:, :R] + a[:, R:]
        return jnp.stack([real, imag])

    first = jnp.concatenate([screened.reshape(-1, 128), free_rows.reshape(-1, 128)])
    rows = gather_rows(first)
    half = nb // 128
    screen_full = to_full_k(rows[:, :half], 2, k_local, cols)
    green_full = to_full_k(rows[:, half:], 2, k_local, cols)
    screen_hat = dft(cosine, sine, screen_full[0], screen_full[1])

    integral, _ = hist_reduce(contract(sigma_of(green_full, HIGHEST), HIGHEST), jnp.zeros((lax.axis_size("mom"),), jnp.float32), hist_n)
    def correction(turn, carry):
        green, integral, deltas = carry
        change = free_rows + step_size * integral - green
        rows = gather_rows(change.reshape(-1, 128))
        mom_sums = jnp.sum(rows * rows, axis=(1, 2))
        full = to_full_k(rows, 2, k_local, cols)
        step, total = hist_reduce(contract(sigma_of(full)), mom_sums, hist_n)
        delta = jnp.sqrt(total / (2.0 * K * R * full_hist))
        deltas = lax.dynamic_update_slice(deltas, delta[None], (turn,))
        green = green + change / (1.0 + delta)
        integral = integral + step / (1.0 + delta)
        return (green, integral, deltas)

    carry = (free_rows, integral, jnp.zeros((ITERS,), jnp.float32))
    for turn in range(ITERS - 1):
        carry = correction(turn, carry)
    green, integral, deltas = carry
    change = free_rows + step_size * integral - green
    local = jnp.sum(change * change)
    n_dev = lax.axis_size(("mom", "hist"))
    spread = jnp.broadcast_to(local, (n_dev, 1))
    total = jnp.sum(lax.all_to_all(spread, ("mom", "hist"), 0, 0, tiled=True))
    delta = jnp.sqrt(total / (2.0 * K * R * full_hist))
    deltas = deltas.at[ITERS - 1].set(delta)
    green = green + change / (1.0 + delta)
    return (green, deltas)


def solution(mesh):
    placed = (
        P(None, "mom", "hist", None),
        P(None, "mom", None, "hist"),
        P(None, "mom", None, "hist"),
    )
    return jax.shard_map(
        shards,
        mesh=mesh,
        in_specs=placed,
        out_specs=(P(None, "mom", None, "hist"), P()),
        check_vma=False,
    )
```

```python
import math

import jax
import jax.numpy as jnp
from jax import lax
from jax.sharding import PartitionSpec as P

K = 128
R = 4
ITERS = 6


step_size = 0.25
HIGHEST = lax.Precision.HIGHEST


def tables(rows):
    points = jnp.arange(K, dtype=jnp.int32)
    product = rows[:, None] * points[None, :] % K
    phase = product.astype(jnp.float32) * (2.0 * math.pi / K)
    return (jnp.cos(phase), jnp.sin(phase))


def mm(table, field, precision=HIGHEST):
    return jnp.dot(table, field, precision=precision)


def dft(cosine, sine, real, imag, precision=HIGHEST):
    both = jnp.concatenate([real, imag], axis=1)
    out = mm(jnp.concatenate([cosine, sine]), both, precision)
    cr = out[: cosine.shape[0]]
    sr = out[cosine.shape[0]:]
    n = real.shape[1]
    return (cr[:, :n] + sr[:, n:], cr[:, n:] - sr[:, :n])


def gather_rows(block):
    n_mom = lax.axis_size("mom")
    return lax.all_to_all(jnp.broadcast_to(block, (n_mom,) + block.shape), "mom", 0, 0, tiled=True)


def to_full_k(rows, lead, k_local, cols):
    g = rows.reshape(rows.shape[0], lead, k_local, R * cols)
    g = jnp.transpose(g, (1, 0, 2, 3))
    return g.reshape(lead, rows.shape[0] * k_local, R * cols)


def hist_reduce(partial, extra, hist_n):
    two, kl, rr, h = partial.shape
    cols = h // hist_n
    x = partial.reshape(two, kl, rr, hist_n, cols)
    x = jnp.transpose(x, (3, 0, 1, 2, 4)).reshape(hist_n, two * kl * rr * cols // 128, 128)
    tile = jnp.pad(extra[None, :], ((0, 7), (0, 128 - extra.shape[0])))
    x = jnp.concatenate([x, jnp.broadcast_to(tile, (hist_n, 8, 128))], axis=1)
    y = lax.all_to_all(x, "hist", 0, 0, tiled=True)
    n = two * kl * rr * cols // 128
    total = jnp.sum(jnp.sum(y[:, n, : extra.shape[0]], axis=0))
    return jnp.sum(y[:, :n], axis=0).reshape(two, kl, rr, cols), total


def shards(hist_panel, free_rows, screened):
    _, k_local, _, cols = free_rows.shape
    hist_n = hist_panel.shape[3] // cols
    full_hist = hist_panel.shape[3]
    mom_i = lax.axis_index("mom")
    cosine, sine = tables(jnp.arange(K, dtype=jnp.int32))
    own = mom_i * k_local + jnp.arange(k_local, dtype=jnp.int32)
    cos_own, sin_own = tables(own)
    cos_own = cos_own / K
    sin_own = sin_own / K
    nb = 2 * k_local * R * cols

    def sigma_of(full, precision=lax.Precision.HIGH):
        hr, hi = dft(cosine, sine, full[0], full[1], precision)
        pr = hr * screen_hat[0] - hi * screen_hat[1]
        pi = hr * screen_hat[1] + hi * screen_hat[0]
        both = jnp.concatenate([pr, pi], axis=1)
        out = mm(jnp.concatenate([cos_own, sin_own]), both, precision)
        cb = out[:k_local]
        sb = out[k_local:]
        n = pr.shape[1]
        back_real = cb[:, :n] - sb[:, n:]
        back_imag = cb[:, n:] + sb[:, :n]
        return jnp.stack([-back_imag, back_real]).reshape(2, k_local, R, cols)

    def contract(sigma, precision):
        x = jnp.concatenate([sigma[0], sigma[1]], axis=1)
        a = jnp.einsum("kxs,kst->kxt", x, hist_panel[0], precision=precision)
        b = jnp.einsum("kxs,kst->kxt", x, hist_panel[1], precision=precision)
        real = a[:, :R] - b[:, R:]
        imag = b[:, :R] + a[:, R:]
        return jnp.stack([real, imag])

    def contract_split(sigma):
        x = jnp.concatenate([sigma[0], sigma[1]], axis=1)
        x_hi = x.astype(jnp.bfloat16)
        x_lo = (x - x_hi.astype(jnp.float32)).astype(jnp.bfloat16)
        both = jnp.concatenate([x_hi, x_lo], axis=1)
        parts = []
        for c in range(2):
            top = jnp.einsum("kxs,kst->kxt", both, panel_hi[c], preferred_element_type=jnp.float32)
            low = jnp.einsum("kxs,kst->kxt", x_hi, panel_lo[c], preferred_element_type=jnp.float32)
            parts.append(top[:, : 2 * R] + top[:, 2 * R:] + low)
        a, b = parts
        real = a[:, :R] - b[:, R:]
        imag = b[:, :R] + a[:, R:]
        return jnp.stack([real, imag])

    first = jnp.concatenate([screened.reshape(-1, 128), free_rows.reshape(-1, 128)])
    rows = gather_rows(first)
    half = nb // 128
    screen_full = to_full_k(rows[:, :half], 2, k_local, cols)
    green_full = to_full_k(rows[:, half:], 2, k_local, cols)
    screen_hat = dft(cosine, sine, screen_full[0], screen_full[1])

    integral, _ = hist_reduce(contract(sigma_of(green_full, HIGHEST), HIGHEST), jnp.zeros((lax.axis_size("mom"),), jnp.float32), hist_n)
    def correction(turn, carry):
        green, integral, deltas = carry
        change = free_rows + step_size * integral - green
        rows = gather_rows(change.reshape(-1, 128))
        mom_sums = jnp.sum(rows * rows, axis=(1, 2))
        full = to_full_k(rows, 2, k_local, cols)
        step, total = hist_reduce(contract_split(sigma_of(full)), mom_sums, hist_n)
        delta = jnp.sqrt(total / (2.0 * K * R * full_hist))
        deltas = lax.dynamic_update_slice(deltas, delta[None], (turn,))
        green = green + change / (1.0 + delta)
        integral = integral + step / (1.0 + delta)
        return (green, integral, deltas)

    panel_hi = hist_panel.astype(jnp.bfloat16)
    panel_lo = (hist_panel - panel_hi.astype(jnp.float32)).astype(jnp.bfloat16)
    carry = (free_rows, integral, jnp.zeros((ITERS,), jnp.float32))
    green, integral, deltas = lax.fori_loop(0, ITERS - 1, correction, carry)
    change = free_rows + step_size * integral - green
    local = jnp.sum(change * change)
    n_dev = lax.axis_size(("mom", "hist"))
    spread = jnp.broadcast_to(local, (n_dev, 1))
    total = jnp.sum(lax.all_to_all(spread, ("mom", "hist"), 0, 0, tiled=True))
    delta = jnp.sqrt(total / (2.0 * K * R * full_hist))
    deltas = deltas.at[ITERS - 1].set(delta)
    green = green + change / (1.0 + delta)
    return (green, deltas)


def solution(mesh):
    placed = (
        P(None, "mom", "hist", None),
        P(None, "mom", None, "hist"),
        P(None, "mom", None, "hist"),
    )
    return jax.shard_map(
        shards,
        mesh=mesh,
        in_specs=placed,
        out_specs=(P(None, "mom", None, "hist"), P()),
        check_vma=False,
    )
```

```python
import math

import jax
import jax.numpy as jnp
from jax import lax
from jax.sharding import PartitionSpec as P

K = 128
R = 4
ITERS = 6


step_size = 0.25
HIGHEST = lax.Precision.HIGHEST


def tables(rows):
    points = jnp.arange(K, dtype=jnp.int32)
    product = rows[:, None] * points[None, :] % K
    phase = product.astype(jnp.float32) * (2.0 * math.pi / K)
    return (jnp.cos(phase), jnp.sin(phase))


def mm(table, field, precision=HIGHEST):
    return jnp.dot(table, field, precision=precision)


def dft(cosine, sine, real, imag, precision=HIGHEST):
    both = jnp.concatenate([real, imag], axis=1)
    out = mm(jnp.concatenate([cosine, sine]), both, precision)
    cr = out[: cosine.shape[0]]
    sr = out[cosine.shape[0]:]
    n = real.shape[1]
    return (cr[:, :n] + sr[:, n:], cr[:, n:] - sr[:, :n])


def gather_rows(block):
    n_mom = lax.axis_size("mom")
    return lax.all_to_all(jnp.broadcast_to(block, (n_mom,) + block.shape), "mom", 0, 0, tiled=True)


def to_full_k(rows, lead, k_local, cols):
    g = rows.reshape(rows.shape[0], lead, k_local, R * cols)
    g = jnp.transpose(g, (1, 0, 2, 3))
    return g.reshape(lead, rows.shape[0] * k_local, R * cols)


def hist_reduce(partial, extra, hist_n):
    two, kl, rr, h = partial.shape
    cols = h // hist_n
    x = partial.reshape(two, kl, rr, hist_n, cols)
    x = jnp.transpose(x, (3, 0, 1, 2, 4)).reshape(hist_n, two * kl * rr * cols // 128, 128)
    tile = jnp.pad(extra[None, :], ((0, 7), (0, 128 - extra.shape[0])))
    x = jnp.concatenate([x, jnp.broadcast_to(tile, (hist_n, 8, 128))], axis=1)
    y = lax.all_to_all(x, "hist", 0, 0, tiled=True)
    n = two * kl * rr * cols // 128
    total = jnp.sum(jnp.sum(y[:, n, : extra.shape[0]], axis=0))
    return jnp.sum(y[:, :n], axis=0).reshape(two, kl, rr, cols), total


def shards(hist_panel, free_rows, screened):
    _, k_local, _, cols = free_rows.shape
    hist_n = hist_panel.shape[3] // cols
    full_hist = hist_panel.shape[3]
    mom_i = lax.axis_index("mom")
    cosine, sine = tables(jnp.arange(K, dtype=jnp.int32))
    own = mom_i * k_local + jnp.arange(k_local, dtype=jnp.int32)
    cos_own, sin_own = tables(own)
    cos_own = cos_own / K
    sin_own = sin_own / K
    nb = 2 * k_local * R * cols

    def sigma_of(full, precision=lax.Precision.HIGH):
        hr, hi = dft(cosine, sine, full[0], full[1], precision)
        pr = hr * screen_hat[0] - hi * screen_hat[1]
        pi = hr * screen_hat[1] + hi * screen_hat[0]
        both = jnp.concatenate([pr, pi], axis=1)
        out = mm(jnp.concatenate([cos_own, sin_own]), both, precision)
        cb = out[:k_local]
        sb = out[k_local:]
        n = pr.shape[1]
        back_real = cb[:, :n] - sb[:, n:]
        back_imag = cb[:, n:] + sb[:, :n]
        return jnp.stack([-back_imag, back_real]).reshape(2, k_local, R, cols)

    def contract_split(sigma):
        x = jnp.concatenate([sigma[0], sigma[1]], axis=1)
        x_hi = x.astype(jnp.bfloat16)
        x_lo = (x - x_hi.astype(jnp.float32)).astype(jnp.bfloat16)
        both = jnp.concatenate([x_hi, x_lo], axis=1)
        parts = []
        for c in range(2):
            top = jnp.einsum("kxs,kst->kxt", both, panel_hi[c], preferred_element_type=jnp.float32)
            low = jnp.einsum("kxs,kst->kxt", x_hi, panel_lo[c], preferred_element_type=jnp.float32)
            parts.append(top[:, : 2 * R] + top[:, 2 * R:] + low)
        a, b = parts
        real = a[:, :R] - b[:, R:]
        imag = b[:, :R] + a[:, R:]
        return jnp.stack([real, imag])

    first = jnp.concatenate([screened.reshape(-1, 128), free_rows.reshape(-1, 128)])
    rows = gather_rows(first)
    half = nb // 128
    screen_full = to_full_k(rows[:, :half], 2, k_local, cols)
    green_full = to_full_k(rows[:, half:], 2, k_local, cols)
    screen_hat = dft(cosine, sine, screen_full[0], screen_full[1])

    panel_hi = hist_panel.astype(jnp.bfloat16)
    panel_lo = (hist_panel - panel_hi.astype(jnp.float32)).astype(jnp.bfloat16)
    integral, _ = hist_reduce(contract_split(sigma_of(green_full, HIGHEST)), jnp.zeros((lax.axis_size("mom"),), jnp.float32), hist_n)
    def correction(turn, carry):
        green, integral, deltas = carry
        change = free_rows + step_size * integral - green
        rows = gather_rows(change.reshape(-1, 128))
        mom_sums = jnp.sum(rows * rows, axis=(1, 2))
        full = to_full_k(rows, 2, k_local, cols)
        step, total = hist_reduce(contract_split(sigma_of(full)), mom_sums, hist_n)
        delta = jnp.sqrt(total / (2.0 * K * R * full_hist))
        deltas = lax.dynamic_update_slice(deltas, delta[None], (turn,))
        green = green + change / (1.0 + delta)
        integral = integral + step / (1.0 + delta)
        return (green, integral, deltas)

    carry = (free_rows, integral, jnp.zeros((ITERS,), jnp.float32))
    green, integral, deltas = lax.fori_loop(0, ITERS - 1, correction, carry)
    change = free_rows + step_size * integral - green
    local = jnp.sum(change * change)
    n_dev = lax.axis_size(("mom", "hist"))
    spread = jnp.broadcast_to(local, (n_dev, 1))
    total = jnp.sum(lax.all_to_all(spread, ("mom", "hist"), 0, 0, tiled=True))
    delta = jnp.sqrt(total / (2.0 * K * R * full_hist))
    deltas = deltas.at[ITERS - 1].set(delta)
    green = green + change / (1.0 + delta)
    return (green, deltas)


def solution(mesh):
    placed = (
        P(None, "mom", "hist", None),
        P(None, "mom", None, "hist"),
        P(None, "mom", None, "hist"),
    )
    return jax.shard_map(
        shards,
        mesh=mesh,
        in_specs=placed,
        out_specs=(P(None, "mom", None, "hist"), P()),
        check_vma=False,
    )
```

```python
import math

import jax
import jax.numpy as jnp
from jax import lax
from jax.sharding import PartitionSpec as P

K = 128
R = 4
ITERS = 6


step_size = 0.25
HIGHEST = lax.Precision.HIGHEST


def tables(rows):
    points = jnp.arange(K, dtype=jnp.int32)
    product = rows[:, None] * points[None, :] % K
    phase = product.astype(jnp.float32) * (2.0 * math.pi / K)
    return (jnp.cos(phase), jnp.sin(phase))


def mm(table, field, precision=HIGHEST):
    return jnp.dot(table, field, precision=precision)


def dft(cosine, sine, real, imag, precision=HIGHEST):
    both = jnp.concatenate([real, imag], axis=1)
    out = mm(jnp.concatenate([cosine, sine]), both, precision)
    cr = out[: cosine.shape[0]]
    sr = out[cosine.shape[0]:]
    n = real.shape[1]
    return (cr[:, :n] + sr[:, n:], cr[:, n:] - sr[:, :n])


def gather_rows(block):
    n_mom = lax.axis_size("mom")
    return lax.all_to_all(jnp.broadcast_to(block, (n_mom,) + block.shape), "mom", 0, 0, tiled=True)


def to_full_k(rows, lead, k_local, cols):
    g = rows.reshape(rows.shape[0], lead, k_local, R * cols)
    g = jnp.transpose(g, (1, 0, 2, 3))
    return g.reshape(lead, rows.shape[0] * k_local, R * cols)


def hist_reduce(partial, extra, hist_n):
    two, kl, rr, h = partial.shape
    cols = h // hist_n
    x = partial.reshape(two, kl, rr, hist_n, cols)
    x = jnp.transpose(x, (3, 0, 1, 2, 4)).reshape(hist_n, two * kl * rr * cols // 128, 128)
    tile = jnp.pad(extra[None, :], ((0, 0), (0, 128 - extra.shape[0])))
    x = jnp.concatenate([x, jnp.broadcast_to(tile, (hist_n, 1, 128))], axis=1)
    y = lax.all_to_all(x, "hist", 0, 0, tiled=True)
    n = two * kl * rr * cols // 128
    total = jnp.sum(jnp.sum(y[:, n, : extra.shape[0]], axis=0))
    return jnp.sum(y[:, :n], axis=0).reshape(two, kl, rr, cols), total


def shards(hist_panel, free_rows, screened):
    _, k_local, _, cols = free_rows.shape
    hist_n = hist_panel.shape[3] // cols
    full_hist = hist_panel.shape[3]
    mom_i = lax.axis_index("mom")
    cosine, sine = tables(jnp.arange(K, dtype=jnp.int32))
    own = mom_i * k_local + jnp.arange(k_local, dtype=jnp.int32)
    cos_own, sin_own = tables(own)
    cos_own = cos_own / K
    sin_own = sin_own / K
    nb = 2 * k_local * R * cols

    def sigma_of(full, precision=lax.Precision.HIGH):
        hr, hi = dft(cosine, sine, full[0], full[1], precision)
        pr = hr * screen_hat[0] - hi * screen_hat[1]
        pi = hr * screen_hat[1] + hi * screen_hat[0]
        both = jnp.concatenate([pr, pi], axis=1)
        out = mm(jnp.concatenate([cos_own, sin_own]), both, precision)
        cb = out[:k_local]
        sb = out[k_local:]
        n = pr.shape[1]
        back_real = cb[:, :n] - sb[:, n:]
        back_imag = cb[:, n:] + sb[:, :n]
        return jnp.stack([-back_imag, back_real]).reshape(2, k_local, R, cols)

    def contract_split(sigma):
        x = jnp.concatenate([sigma[0], sigma[1]], axis=1)
        x_hi = x.astype(jnp.bfloat16)
        x_lo = (x - x_hi.astype(jnp.float32)).astype(jnp.bfloat16)
        both = jnp.concatenate([x_hi, x_lo], axis=1)
        parts = []
        for c in range(2):
            top = jnp.einsum("kxs,kst->kxt", both, panel_hi[c], preferred_element_type=jnp.float32)
            low = jnp.einsum("kxs,kst->kxt", x_hi, panel_lo[c], preferred_element_type=jnp.float32)
            parts.append(top[:, : 2 * R] + top[:, 2 * R:] + low)
        a, b = parts
        real = a[:, :R] - b[:, R:]
        imag = b[:, :R] + a[:, R:]
        return jnp.stack([real, imag])

    first = jnp.concatenate([screened.reshape(-1, 128), free_rows.reshape(-1, 128)])
    rows = gather_rows(first)
    half = nb // 128
    screen_full = to_full_k(rows[:, :half], 2, k_local, cols)
    green_full = to_full_k(rows[:, half:], 2, k_local, cols)
    screen_hat = dft(cosine, sine, screen_full[0], screen_full[1])

    panel_hi = hist_panel.astype(jnp.bfloat16)
    panel_lo = (hist_panel - panel_hi.astype(jnp.float32)).astype(jnp.bfloat16)
    integral, _ = hist_reduce(contract_split(sigma_of(green_full, HIGHEST)), jnp.zeros((lax.axis_size("mom"),), jnp.float32), hist_n)
    def correction(turn, carry):
        green, integral, deltas = carry
        change = free_rows + step_size * integral - green
        rows = gather_rows(change.reshape(-1, 128))
        mom_sums = jnp.sum(rows * rows, axis=(1, 2))
        full = to_full_k(rows, 2, k_local, cols)
        step, total = hist_reduce(contract_split(sigma_of(full)), mom_sums, hist_n)
        delta = jnp.sqrt(total / (2.0 * K * R * full_hist))
        deltas = lax.dynamic_update_slice(deltas, delta[None], (turn,))
        green = green + change / (1.0 + delta)
        integral = integral + step / (1.0 + delta)
        return (green, integral, deltas)

    carry = (free_rows, integral, jnp.zeros((ITERS,), jnp.float32))
    green, integral, deltas = lax.fori_loop(0, ITERS - 1, correction, carry)
    change = free_rows + step_size * integral - green
    local = jnp.sum(change * change)
    n_dev = lax.axis_size(("mom", "hist"))
    spread = jnp.broadcast_to(local, (n_dev, 1))
    total = jnp.sum(lax.all_to_all(spread, ("mom", "hist"), 0, 0, tiled=True))
    delta = jnp.sqrt(total / (2.0 * K * R * full_hist))
    deltas = deltas.at[ITERS - 1].set(delta)
    green = green + change / (1.0 + delta)
    return (green, deltas)


def solution(mesh):
    placed = (
        P(None, "mom", "hist", None),
        P(None, "mom", None, "hist"),
        P(None, "mom", None, "hist"),
    )
    return jax.shard_map(
        shards,
        mesh=mesh,
        in_specs=placed,
        out_specs=(P(None, "mom", None, "hist"), P()),
        check_vma=False,
    )
```

```python
import math

import jax
import jax.numpy as jnp
from jax import lax
from jax.sharding import PartitionSpec as P

K = 128
R = 4
ITERS = 6


step_size = 0.25
HIGHEST = lax.Precision.HIGHEST


def tables(rows):
    points = jnp.arange(K, dtype=jnp.int32)
    product = rows[:, None] * points[None, :] % K
    phase = product.astype(jnp.float32) * (2.0 * math.pi / K)
    return (jnp.cos(phase), jnp.sin(phase))


def mm(table, field, precision=HIGHEST):
    return jnp.dot(table, field, precision=precision)


def dft(cosine, sine, real, imag, precision=HIGHEST):
    both = jnp.concatenate([real, imag], axis=1)
    out = mm(jnp.concatenate([cosine, sine]), both, precision)
    cr = out[: cosine.shape[0]]
    sr = out[cosine.shape[0]:]
    n = real.shape[1]
    return (cr[:, :n] + sr[:, n:], cr[:, n:] - sr[:, :n])


def gather_rows(block):
    n_mom = lax.axis_size("mom")
    return lax.all_to_all(jnp.broadcast_to(block, (n_mom,) + block.shape), "mom", 0, 0, tiled=True)


def to_full_k(rows, lead, k_local, cols):
    g = rows.reshape(rows.shape[0], lead, k_local, R * cols)
    g = jnp.transpose(g, (1, 0, 2, 3))
    return g.reshape(lead, rows.shape[0] * k_local, R * cols)


def hist_reduce(partial, extra, hist_n):
    two, kl, rr, h = partial.shape
    cols = h // hist_n
    x = partial.reshape(two, kl, rr, hist_n, cols)
    x = jnp.transpose(x, (3, 0, 1, 2, 4)).reshape(hist_n, two * kl * rr * cols // 128, 128)
    tile = jnp.pad(extra[None, :], ((0, 0), (0, 128 - extra.shape[0])))
    x = jnp.concatenate([x, jnp.broadcast_to(tile, (hist_n, 1, 128))], axis=1)
    y = lax.all_to_all(x, "hist", 0, 0, tiled=True)
    n = two * kl * rr * cols // 128
    total = jnp.sum(jnp.sum(y[:, n, : extra.shape[0]], axis=0))
    return jnp.sum(y[:, :n], axis=0).reshape(two, kl, rr, cols), total


def shards(hist_panel, free_rows, screened):
    _, k_local, _, cols = free_rows.shape
    hist_n = hist_panel.shape[3] // cols
    full_hist = hist_panel.shape[3]
    mom_i = lax.axis_index("mom")
    cosine, sine = tables(jnp.arange(K, dtype=jnp.int32))
    own = mom_i * k_local + jnp.arange(k_local, dtype=jnp.int32)
    cos_own, sin_own = tables(own)
    cos_own = cos_own / K
    sin_own = sin_own / K
    nb = 2 * k_local * R * cols

    def sigma_of(full, precision=lax.Precision.HIGH):
        hr, hi = dft(cosine, sine, full[0], full[1], precision)
        pr = hr * screen_hat[0] - hi * screen_hat[1]
        pi = hr * screen_hat[1] + hi * screen_hat[0]
        both = jnp.concatenate([pr, pi], axis=1)
        out = mm(jnp.concatenate([cos_own, sin_own]), both, precision)
        cb = out[:k_local]
        sb = out[k_local:]
        n = pr.shape[1]
        back_real = cb[:, :n] - sb[:, n:]
        back_imag = cb[:, n:] + sb[:, :n]
        return jnp.stack([-back_imag, back_real]).reshape(2, k_local, R, cols)

    def contract_split(sigma):
        x = jnp.concatenate([sigma[0], sigma[1]], axis=1)
        x_hi = x.astype(jnp.bfloat16)
        x_lo = (x - x_hi.astype(jnp.float32)).astype(jnp.bfloat16)
        both = jnp.concatenate([x_hi, x_lo], axis=1)
        parts = []
        for c in range(2):
            top = jnp.einsum("kxs,kst->kxt", both, panel_hi[c], preferred_element_type=jnp.float32)
            low = jnp.einsum("kxs,kst->kxt", x_hi, panel_lo[c], preferred_element_type=jnp.float32)
            parts.append(top[:, : 2 * R] + top[:, 2 * R:] + low)
        a, b = parts
        real = a[:, :R] - b[:, R:]
        imag = b[:, :R] + a[:, R:]
        return jnp.stack([real, imag])

    first = jnp.concatenate([screened.reshape(-1, 128), free_rows.reshape(-1, 128)])
    rows = gather_rows(first)
    half = nb // 128
    screen_full = to_full_k(rows[:, :half], 2, k_local, cols)
    green_full = to_full_k(rows[:, half:], 2, k_local, cols)
    screen_hat = dft(cosine, sine, screen_full[0], screen_full[1])

    panel_hi = hist_panel.astype(jnp.bfloat16)
    panel_lo = (hist_panel - panel_hi.astype(jnp.float32)).astype(jnp.bfloat16)
    integral, _ = hist_reduce(contract_split(sigma_of(green_full, HIGHEST)), jnp.zeros((lax.axis_size("mom"),), jnp.float32), hist_n)
    def correction(turn, carry):
        green, integral, deltas = carry
        change = free_rows + step_size * integral - green
        rows = gather_rows(change.reshape(-1, 128))
        mom_sums = jnp.sum(rows * rows, axis=(1, 2))
        full = to_full_k(rows, 2, k_local, cols)
        step, total = hist_reduce(contract_split(sigma_of(full)), mom_sums, hist_n)
        delta = jnp.sqrt(total / (2.0 * K * R * full_hist))
        deltas = lax.dynamic_update_slice(deltas, delta[None], (turn,))
        green = green + change / (1.0 + delta)
        integral = integral + step / (1.0 + delta)
        return (green, integral, deltas)

    carry = (free_rows, integral, jnp.zeros((ITERS,), jnp.float32))
    for turn in range(ITERS - 1):
        carry = correction(turn, carry)
    green, integral, deltas = carry
    change = free_rows + step_size * integral - green
    local = jnp.sum(change * change)
    n_dev = lax.axis_size(("mom", "hist"))
    spread = jnp.broadcast_to(local, (n_dev, 1))
    total = jnp.sum(lax.all_to_all(spread, ("mom", "hist"), 0, 0, tiled=True))
    delta = jnp.sqrt(total / (2.0 * K * R * full_hist))
    deltas = deltas.at[ITERS - 1].set(delta)
    green = green + change / (1.0 + delta)
    return (green, deltas)


def solution(mesh):
    placed = (
        P(None, "mom", "hist", None),
        P(None, "mom", None, "hist"),
        P(None, "mom", None, "hist"),
    )
    return jax.shard_map(
        shards,
        mesh=mesh,
        in_specs=placed,
        out_specs=(P(None, "mom", None, "hist"), P()),
        check_vma=False,
    )
```

```python
import math

import jax
import jax.numpy as jnp
from jax import lax
from jax.sharding import PartitionSpec as P

K = 128
R = 4
ITERS = 6


step_size = 0.25
HIGHEST = lax.Precision.HIGHEST


def tables(rows):
    points = jnp.arange(K, dtype=jnp.int32)
    product = rows[:, None] * points[None, :] % K
    phase = product.astype(jnp.float32) * (2.0 * math.pi / K)
    return (jnp.cos(phase), jnp.sin(phase))


def mm(table, field, precision=HIGHEST):
    return jnp.dot(table, field, precision=precision)


def dft(cosine, sine, real, imag, precision=HIGHEST):
    both = jnp.concatenate([real, imag], axis=1)
    out = mm(jnp.concatenate([cosine, sine]), both, precision)
    cr = out[: cosine.shape[0]]
    sr = out[cosine.shape[0]:]
    n = real.shape[1]
    return (cr[:, :n] + sr[:, n:], cr[:, n:] - sr[:, :n])


def gather_rows(block):
    n_mom = lax.axis_size("mom")
    return lax.all_to_all(jnp.broadcast_to(block, (n_mom,) + block.shape), "mom", 0, 0, tiled=True)


def to_full_k(rows, lead, k_local, cols):
    g = rows.reshape(rows.shape[0], lead, k_local, R * cols)
    g = jnp.transpose(g, (1, 0, 2, 3))
    return g.reshape(lead, rows.shape[0] * k_local, R * cols)


def hist_reduce(partial, extra, hist_n):
    _, two, kl, rr, cols = partial.shape
    x = partial.reshape(hist_n, two * kl * rr * cols // 128, 128)
    tile = jnp.pad(extra[None, :], ((0, 0), (0, 128 - extra.shape[0])))
    x = jnp.concatenate([x, jnp.broadcast_to(tile, (hist_n, 1, 128))], axis=1)
    y = lax.all_to_all(x, "hist", 0, 0, tiled=True)
    n = two * kl * rr * cols // 128
    total = jnp.sum(jnp.sum(y[:, n, : extra.shape[0]], axis=0))
    return jnp.sum(y[:, :n], axis=0).reshape(two, kl, rr, cols), total


def shards(hist_panel, free_rows, screened):
    _, k_local, _, cols = free_rows.shape
    hist_n = hist_panel.shape[3] // cols
    full_hist = hist_panel.shape[3]
    mom_i = lax.axis_index("mom")
    cosine, sine = tables(jnp.arange(K, dtype=jnp.int32))
    own = mom_i * k_local + jnp.arange(k_local, dtype=jnp.int32)
    cos_own, sin_own = tables(own)
    cos_own = cos_own / K
    sin_own = sin_own / K
    nb = 2 * k_local * R * cols

    def sigma_of(full, precision=lax.Precision.HIGH):
        hr, hi = dft(cosine, sine, full[0], full[1], precision)
        pr = hr * screen_hat[0] - hi * screen_hat[1]
        pi = hr * screen_hat[1] + hi * screen_hat[0]
        both = jnp.concatenate([pr, pi], axis=1)
        out = mm(jnp.concatenate([cos_own, sin_own]), both, precision)
        cb = out[:k_local]
        sb = out[k_local:]
        n = pr.shape[1]
        back_real = cb[:, :n] - sb[:, n:]
        back_imag = cb[:, n:] + sb[:, :n]
        return jnp.stack([-back_imag, back_real]).reshape(2, k_local, R, cols)

    def contract_split(sigma):
        x = jnp.concatenate([sigma[0], sigma[1]], axis=1)
        x_hi = x.astype(jnp.bfloat16)
        x_lo = (x - x_hi.astype(jnp.float32)).astype(jnp.bfloat16)
        both = jnp.concatenate([x_hi, x_lo], axis=1)
        parts = []
        for c in range(2):
            top = jnp.einsum("kxs,kshu->hkxu", both, panel_hi[c], preferred_element_type=jnp.float32)
            low = jnp.einsum("kxs,kshu->hkxu", x_hi, panel_lo[c], preferred_element_type=jnp.float32)
            parts.append(top[:, :, : 2 * R] + top[:, :, 2 * R:] + low)
        a, b = parts
        real = a[:, :, :R] - b[:, :, R:]
        imag = b[:, :, :R] + a[:, :, R:]
        return jnp.stack([real, imag], axis=1)

    first = jnp.concatenate([screened.reshape(-1, 128), free_rows.reshape(-1, 128)])
    rows = gather_rows(first)
    half = nb // 128
    screen_full = to_full_k(rows[:, :half], 2, k_local, cols)
    green_full = to_full_k(rows[:, half:], 2, k_local, cols)
    screen_hat = dft(cosine, sine, screen_full[0], screen_full[1])

    panel = hist_panel.reshape(hist_panel.shape[:3] + (hist_n, cols))
    panel_hi = panel.astype(jnp.bfloat16)
    panel_lo = (panel - panel_hi.astype(jnp.float32)).astype(jnp.bfloat16)
    integral, _ = hist_reduce(contract_split(sigma_of(green_full, HIGHEST)), jnp.zeros((lax.axis_size("mom"),), jnp.float32), hist_n)
    def correction(turn, carry):
        green, integral, deltas = carry
        change = free_rows + step_size * integral - green
        rows = gather_rows(change.reshape(-1, 128))
        mom_sums = jnp.sum(rows * rows, axis=(1, 2))
        full = to_full_k(rows, 2, k_local, cols)
        step, total = hist_reduce(contract_split(sigma_of(full)), mom_sums, hist_n)
        delta = jnp.sqrt(total / (2.0 * K * R * full_hist))
        deltas = lax.dynamic_update_slice(deltas, delta[None], (turn,))
        green = green + change / (1.0 + delta)
        integral = integral + step / (1.0 + delta)
        return (green, integral, deltas)

    carry = (free_rows, integral, jnp.zeros((ITERS,), jnp.float32))
    for turn in range(ITERS - 1):
        carry = correction(turn, carry)
    green, integral, deltas = carry
    change = free_rows + step_size * integral - green
    local = jnp.sum(change * change)
    n_dev = lax.axis_size(("mom", "hist"))
    spread = jnp.broadcast_to(local, (n_dev, 1))
    total = jnp.sum(lax.all_to_all(spread, ("mom", "hist"), 0, 0, tiled=True))
    delta = jnp.sqrt(total / (2.0 * K * R * full_hist))
    deltas = deltas.at[ITERS - 1].set(delta)
    green = green + change / (1.0 + delta)
    return (green, deltas)


def solution(mesh):
    placed = (
        P(None, "mom", "hist", None),
        P(None, "mom", None, "hist"),
        P(None, "mom", None, "hist"),
    )
    return jax.shard_map(
        shards,
        mesh=mesh,
        in_specs=placed,
        out_specs=(P(None, "mom", None, "hist"), P()),
        check_vma=False,
    )
```

```python
import math

import jax
import jax.numpy as jnp
from jax import lax
from jax.sharding import PartitionSpec as P

K = 128
R = 4
ITERS = 6


step_size = 0.25
HIGHEST = lax.Precision.HIGHEST


def tables(rows):
    points = jnp.arange(K, dtype=jnp.int32)
    product = rows[:, None] * points[None, :] % K
    phase = product.astype(jnp.float32) * (2.0 * math.pi / K)
    return (jnp.cos(phase), jnp.sin(phase))


def mm(table, field, precision=HIGHEST):
    return jnp.dot(table, field, precision=precision)


def dft(cosine, sine, real, imag, precision=HIGHEST):
    both = jnp.concatenate([real, imag], axis=1)
    out = mm(jnp.concatenate([cosine, sine]), both, precision)
    cr = out[: cosine.shape[0]]
    sr = out[cosine.shape[0]:]
    n = real.shape[1]
    return (cr[:, :n] + sr[:, n:], cr[:, n:] - sr[:, :n])


def gather_rows(block):
    n_mom = lax.axis_size("mom")
    return lax.all_to_all(jnp.broadcast_to(block, (n_mom,) + block.shape), "mom", 0, 0, tiled=True)


def to_full_k(rows, lead, k_local, cols):
    g = rows.reshape(rows.shape[0], lead, k_local, R * cols)
    g = jnp.transpose(g, (1, 0, 2, 3))
    return g.reshape(lead, rows.shape[0] * k_local, R * cols)


def hist_reduce(partial, extra, hist_n):
    two, kl, rr, h = partial.shape
    cols = h // hist_n
    x = partial.reshape(two, kl, rr, hist_n, cols)
    x = jnp.transpose(x, (3, 0, 1, 2, 4)).reshape(hist_n, two * kl * rr * cols // 128, 128)
    tile = jnp.pad(extra[None, :], ((0, 0), (0, 128 - extra.shape[0])))
    x = jnp.concatenate([x, jnp.broadcast_to(tile, (hist_n, 1, 128))], axis=1)
    y = lax.all_to_all(x, "hist", 0, 0, tiled=True)
    n = two * kl * rr * cols // 128
    total = jnp.sum(jnp.sum(y[:, n, : extra.shape[0]], axis=0))
    return jnp.sum(y[:, :n], axis=0).reshape(two, kl, rr, cols), total


def shards(hist_panel, free_rows, screened):
    _, k_local, _, cols = free_rows.shape
    hist_n = hist_panel.shape[3] // cols
    full_hist = hist_panel.shape[3]
    mom_i = lax.axis_index("mom")
    cosine, sine = tables(jnp.arange(K, dtype=jnp.int32))
    own = mom_i * k_local + jnp.arange(k_local, dtype=jnp.int32)
    cos_own, sin_own = tables(own)
    cos_own = cos_own / K
    sin_own = sin_own / K
    nb = 2 * k_local * R * cols

    def sigma_of(full, precision=lax.Precision.HIGH, hat=None):
        hr, hi = dft(cosine, sine, full[0], full[1], precision) if hat is None else hat
        pr = hr * screen_hat[0] - hi * screen_hat[1]
        pi = hr * screen_hat[1] + hi * screen_hat[0]
        both = jnp.concatenate([pr, pi], axis=1)
        out = mm(jnp.concatenate([cos_own, sin_own]), both, precision)
        cb = out[:k_local]
        sb = out[k_local:]
        n = pr.shape[1]
        back_real = cb[:, :n] - sb[:, n:]
        back_imag = cb[:, n:] + sb[:, :n]
        return jnp.stack([-back_imag, back_real]).reshape(2, k_local, R, cols)

    def contract_split(sigma):
        x = jnp.concatenate([sigma[0], sigma[1]], axis=1)
        x_hi = x.astype(jnp.bfloat16)
        x_lo = (x - x_hi.astype(jnp.float32)).astype(jnp.bfloat16)
        both = jnp.concatenate([x_hi, x_lo], axis=1)
        parts = []
        for c in range(2):
            top = jnp.einsum("kxs,kst->kxt", both, panel_hi[c], preferred_element_type=jnp.float32)
            low = jnp.einsum("kxs,kst->kxt", x_hi, panel_lo[c], preferred_element_type=jnp.float32)
            parts.append(top[:, : 2 * R] + top[:, 2 * R:] + low)
        a, b = parts
        real = a[:, :R] - b[:, R:]
        imag = b[:, :R] + a[:, R:]
        return jnp.stack([real, imag])

    first = jnp.concatenate([screened.reshape(-1, 128), free_rows.reshape(-1, 128)])
    rows = gather_rows(first)
    half = nb // 128
    screen_full = to_full_k(rows[:, :half], 2, k_local, cols)
    green_full = to_full_k(rows[:, half:], 2, k_local, cols)
    wide = R * cols
    hr, hi = dft(cosine, sine, jnp.concatenate([screen_full[0], green_full[0]], axis=1),
                 jnp.concatenate([screen_full[1], green_full[1]], axis=1))
    screen_hat = (hr[:, :wide], hi[:, :wide])
    green_hat = (hr[:, wide:], hi[:, wide:])

    panel_hi = hist_panel.astype(jnp.bfloat16)
    panel_lo = (hist_panel - panel_hi.astype(jnp.float32)).astype(jnp.bfloat16)
    integral, _ = hist_reduce(contract_split(sigma_of(green_full, HIGHEST, green_hat)), jnp.zeros((lax.axis_size("mom"),), jnp.float32), hist_n)
    def correction(turn, carry):
        green, integral, deltas = carry
        change = free_rows + step_size * integral - green
        rows = gather_rows(change.reshape(-1, 128))
        mom_sums = jnp.sum(rows * rows, axis=(1, 2))
        full = to_full_k(rows, 2, k_local, cols)
        step, total = hist_reduce(contract_split(sigma_of(full)), mom_sums, hist_n)
        delta = jnp.sqrt(total / (2.0 * K * R * full_hist))
        deltas = lax.dynamic_update_slice(deltas, delta[None], (turn,))
        green = green + change / (1.0 + delta)
        integral = integral + step / (1.0 + delta)
        return (green, integral, deltas)

    carry = (free_rows, integral, jnp.zeros((ITERS,), jnp.float32))
    for turn in range(ITERS - 1):
        carry = correction(turn, carry)
    green, integral, deltas = carry
    change = free_rows + step_size * integral - green
    local = jnp.sum(change * change)
    n_dev = lax.axis_size(("mom", "hist"))
    spread = jnp.broadcast_to(local, (n_dev, 1))
    total = jnp.sum(lax.all_to_all(spread, ("mom", "hist"), 0, 0, tiled=True))
    delta = jnp.sqrt(total / (2.0 * K * R * full_hist))
    deltas = deltas.at[ITERS - 1].set(delta)
    green = green + change / (1.0 + delta)
    return (green, deltas)


def solution(mesh):
    placed = (
        P(None, "mom", "hist", None),
        P(None, "mom", None, "hist"),
        P(None, "mom", None, "hist"),
    )
    return jax.shard_map(
        shards,
        mesh=mesh,
        in_specs=placed,
        out_specs=(P(None, "mom", None, "hist"), P()),
        check_vma=False,
    )
```
